512 devices in a mesh: ulysses: 8 (over z_hi, x), context: 64 (over y, z_lo, core).
Axes of the slice: x: 4, y: 8, z: 8 (z_hi: 2, z_lo: 4; z = z_hi * 4 + z_lo), core: 2. Of those that a mesh axis runs over, the one named last changes fastest.
Arguments:
- queries: bfloat16 [49152, 5120], P(('context', 'ulysses')), may hold values from -7 to 7
- key_vectors: bfloat16 [49152, 5120], P(('context', 'ulysses')), may hold values from -7 to 7
- value_vectors: bfloat16 [49152, 5120], P(('context', 'ulysses')), may hold values from -6 to 6
- labels: int32 [40], replicated, may hold values from 0 to 1, as said below
- block_lists: int32 [40, 768, 5], replicated, may hold values from 0 to 767, as said below
- counts: int32 [40, 768], replicated, may hold values from 1 to 5, as said below
- query_scale: float32 [40], replicated, may hold values from 1.5 to 3
- key_scale: float32 [40], replicated, may hold values from 1.5 to 3
- value_scale: float32 [40], replicated, may hold values from 0.5 to 2
Outputs:
- attended: bfloat16 [49152, 5120], P(('context', 'ulysses'))
The draws below stay inside these ranges and needn't reach their ends.
Inputs may be any that keep to these rules, and one draw needn't show every extreme that they name: `labels`: exactly 16 entries are 1, the others 0; every aligned run of 5 heads holds at least one 0. Every entry of block_lists[h, b] lies within 2 blocks of b; the first entry is b itself and the first counts[h, b] entries are distinct. counts[h, b] is at least one less than and at most the number of blocks of the clip within 2 blocks of b; every head has a query block that uses all 5 entries.
All inputs are finite; a program needn't handle non-finite values.
Results may differ from the reference program's by a relative error of at most 0.0024.
Values may be sent and summed in bfloat16 or wider, within the bound.
No kernel may reach another device: no remote copies, remote signals or barrier semaphores. Data moves between devices by JAX's collectives and lax.ppermute only.
A program may use at most 128 MiB of HBM per device.

```python
import math
import jax
import jax.numpy as jnp
from jax import lax

HEADS = 40
HEAD_DIM = 128
FRAMES = 16
TEMPORAL = 16
MARGIN = 2
BLOCK = 64
HEADS_DEV = 5
POSITIONS = 3072
SEQ = 49152
SHARD_BLOCKS = 12
QUERY_BLOCKS = 768
KEY_BLOCKS = 5


def make_labels(key):
    first_key, second_key = jax.random.split(key)
    group_raw = jax.random.randint(first_key, (HEADS // HEADS_DEV, HEADS_DEV), 0, 2 ** 20)
    group_scores = group_raw * HEADS_DEV + jnp.arange(HEADS_DEV, dtype=jnp.int32)[None, :]
    group_ranks = jnp.argsort(jnp.argsort(group_scores, axis=1), axis=1)
    forced = (group_ranks == 0).reshape(HEADS)
    head_iota = jnp.arange(HEADS, dtype=jnp.int32)
    raw = jax.random.randint(second_key, (HEADS,), 0, 2 ** 20)
    scores = raw * HEADS + head_iota
    scores = jnp.where(forced, -1 - head_iota, scores)
    ranking = jnp.argsort(jnp.argsort(-scores))
    return (ranking < TEMPORAL).astype(jnp.int32)


def draw_labels(key, part):
    return make_labels(jax.random.fold_in(key, 11))


def list_parts(key):
    offsets = jnp.arange(KEY_BLOCKS, dtype=jnp.int32) - MARGIN
    query_ids = jnp.arange(QUERY_BLOCKS, dtype=jnp.int32)
    candidate = query_ids[:, None] + offsets[None, :]
    inside = (candidate >= 0) & (candidate < QUERY_BLOCKS)
    allowed = jnp.broadcast_to(inside[None], (HEADS, QUERY_BLOCKS, KEY_BLOCKS))
    return (query_ids, offsets, candidate, allowed)


def draw_block_lists(key, part):
    query_ids, offsets, candidate, allowed = list_parts(key)
    index_row = jnp.arange(KEY_BLOCKS, dtype=jnp.int32)
    raw = jax.random.randint(jax.random.fold_in(key, 12), (HEADS, QUERY_BLOCKS, KEY_BLOCKS), 0, 2 ** 20)
    scores = raw * KEY_BLOCKS + index_row
    scores = jnp.where((offsets == 0)[None, None, :], 2 ** 30, scores)
    scores = jnp.where(allowed, scores, -1 - index_row)
    _, picked = lax.top_k(scores, KEY_BLOCKS)
    full_candidate = jnp.broadcast_to(candidate[None], (HEADS, QUERY_BLOCKS, KEY_BLOCKS))
    picked_candidate = jnp.take_along_axis(full_candidate, picked, axis=2)
    picked_allowed = jnp.take_along_axis(allowed, picked, axis=2)
    return jnp.where(picked_allowed, picked_candidate, query_ids[None, :, None]).astype(jnp.int32)


def draw_counts(key, part):
    query_ids, offsets, candidate, allowed = list_parts(key)
    room = jnp.sum(allowed.astype(jnp.int32), axis=-1)
    first_key, second_key = jax.random.split(jax.random.fold_in(key, 13))
    lowest = jnp.maximum(room - 1, 1)
    drawn = jax.random.randint(first_key, (HEADS, QUERY_BLOCKS), lowest, room + 1)
    chosen = jax.random.randint(second_key, (HEADS, 1), MARGIN, QUERY_BLOCKS - MARGIN)
    full_row = query_ids[None, :] == chosen
    return jnp.where(full_row, room, drawn).astype(jnp.int32)


def draw_queries(key, part):
    base_key = jax.random.fold_in(key, 21)
    drawn = jnp.clip(jax.random.normal(base_key, (SEQ, HEADS, HEAD_DIM)), -6.0, 6.0)
    return drawn.reshape(SEQ, HEADS * HEAD_DIM).astype(jnp.bfloat16)


def draw_key_vectors(key, part):
    base_key = jax.random.fold_in(key, 22)
    drawn = jnp.clip(jax.random.normal(base_key, (SEQ, HEADS, HEAD_DIM)), -6.0, 6.0)
    return drawn.reshape(SEQ, HEADS * HEAD_DIM).astype(jnp.bfloat16)


def steps_of(stream_key, dims, pieces, low, high):
    factor_of = 1.0
    for axis_at, parts in pieces:
        draws = jax.random.uniform(jax.random.fold_in(jax.random.fold_in(stream_key, 6), axis_at), (parts,), jnp.float32, low / len(pieces), high / len(pieces))
        factor_of = factor_of * jnp.repeat(jnp.exp(draws), dims[axis_at] // parts).reshape((-1,) + (1,) * (len(dims) - 1 - axis_at))
    return factor_of


def noise(rng, shape, width, most, cuts=(), held_as=jnp.bfloat16):
    values = width * jax.random.normal(rng, shape, jnp.float32)
    if cuts:
        values = values * steps_of(rng, shape, cuts, -0.22, 0.18)
    return jnp.clip(values, -most, most).astype(held_as)


def setup_inputs(seed: int = 0) -> dict:
    key_of = jax.random.split(jax.random.key(seed), 10)
    queries = draw_queries(jax.random.fold_in(key_of[9], 71), 0)
    key_vectors = draw_key_vectors(jax.random.fold_in(key_of[9], 71), 0)
    value_vectors = noise(key_of[2], (SEQ, HEADS * HEAD_DIM), 1.0, 6.0, ((0, 512),))
    labels = draw_labels(jax.random.fold_in(key_of[9], 71), 0)
    block_lists = draw_block_lists(jax.random.fold_in(key_of[9], 71), 0)
    counts = draw_counts(jax.random.fold_in(key_of[9], 71), 0)
    query_scale = jnp.clip(jnp.exp(jax.random.uniform(key_of[6], (HEADS,), jnp.float32, math.log(1.5), math.log(3.0))), 1.5, 3.0)
    key_scale = jnp.clip(jnp.exp(jax.random.uniform(key_of[7], (HEADS,), jnp.float32, math.log(1.5), math.log(3.0))), 1.5, 3.0)
    value_scale = jnp.clip(jnp.exp(jax.random.uniform(key_of[8], (HEADS,), jnp.float32, math.log(0.5), math.log(2.0))), 0.5, 2.0)
    return {"queries": queries, "key_vectors": key_vectors, "value_vectors": value_vectors, "labels": labels, "block_lists": block_lists, "counts": counts, "query_scale": query_scale, "key_scale": key_scale, "value_scale": value_scale}


def reorder(column, temporal):
    position_major = column.reshape(FRAMES, POSITIONS, HEAD_DIM).transpose(1, 0, 2).reshape(SEQ, HEAD_DIM)
    return jnp.where(temporal == 1, position_major, column)

def restore(column, temporal):
    frame_major = column.reshape(POSITIONS, FRAMES, HEAD_DIM).transpose(1, 0, 2).reshape(SEQ, HEAD_DIM)
    return jnp.where(temporal == 1, frame_major, column)

def group_attend(query_tiles, key_blocks, value_blocks, chosen, allowed, logit_scale, value_factor):
    group = query_tiles.shape[0]
    collected_keys = key_blocks[chosen].reshape(group, KEY_BLOCKS * BLOCK, HEAD_DIM)
    collected_values = value_blocks[chosen].reshape(group, KEY_BLOCKS * BLOCK, HEAD_DIM)
    attention_logits = jnp.einsum('fac,foc->fao', query_tiles.astype(jnp.float32), collected_keys.astype(jnp.float32), precision=lax.Precision.HIGHEST) * logit_scale
    valid = jnp.repeat(jnp.arange(KEY_BLOCKS)[None, :] < allowed[:, None], BLOCK, axis=1)
    attention_logits = jnp.where(valid[:, None, :], attention_logits, -jnp.inf)
    peak = lax.optimization_barrier(jnp.max(attention_logits, axis=-1, keepdims=True))
    weight = jnp.exp(attention_logits - peak)
    total = lax.optimization_barrier(jnp.sum(weight, axis=-1, keepdims=True))
    weight_second = lax.optimization_barrier(weight.astype(jnp.bfloat16))
    blended_output = jnp.einsum('oem,omg->oeg', weight_second.astype(jnp.float32), collected_values.astype(jnp.float32), precision=lax.Precision.HIGHEST)
    return (blended_output * (value_factor / total)).astype(jnp.bfloat16)

def reference(queries, key_vectors, value_vectors, labels, block_lists, counts, query_scale, key_scale, value_scale):
    group_count = QUERY_BLOCKS // SHARD_BLOCKS

    def one_head(head_index):
        temporal = labels[head_index]
        start = head_index * HEAD_DIM
        query_column = reorder(lax.dynamic_slice_in_dim(queries, start, HEAD_DIM, 1), temporal)
        key_column = reorder(lax.dynamic_slice_in_dim(key_vectors, start, HEAD_DIM, 1), temporal)
        value_column = reorder(lax.dynamic_slice_in_dim(value_vectors, start, HEAD_DIM, 1), temporal)
        query_groups = query_column.reshape(group_count, SHARD_BLOCKS, BLOCK, HEAD_DIM)
        key_blocks = key_column.reshape(QUERY_BLOCKS, BLOCK, HEAD_DIM)
        value_blocks = value_column.reshape(QUERY_BLOCKS, BLOCK, HEAD_DIM)
        list_groups = block_lists[head_index].reshape(group_count, SHARD_BLOCKS, KEY_BLOCKS)
        count_groups = counts[head_index].reshape(group_count, SHARD_BLOCKS)
        logit_scale = query_scale[head_index] * key_scale[head_index] / math.sqrt(HEAD_DIM)
        value_factor = value_scale[head_index]

        def per_group(items):
            return group_attend(items[0], key_blocks, value_blocks, items[1], items[2], logit_scale, value_factor)
        outputs = lax.map(per_group, (query_groups, list_groups, count_groups))
        return restore(outputs.reshape(SEQ, HEAD_DIM), temporal)
    result = lax.map(one_head, jnp.arange(HEADS, dtype=jnp.int32))
    return result.transpose(1, 0, 2).reshape(SEQ, HEADS * HEAD_DIM)
```

```python
import math

import jax
import jax.numpy as jnp
from jax import lax
from jax.sharding import Mesh, PartitionSpec as P

FRAMES = 16
MARGIN = 2
BLOCK = 64


def with_halo(cells, axes, order):
    width = MARGIN * BLOCK
    pairs = list(zip(order[:-1], order[1:]))
    lower = lax.ppermute(cells[-width:], axes, pairs)
    upper = lax.ppermute(cells[:width], axes, [(b, a) for a, b in pairs])
    return jnp.concatenate([lower, cells, upper], axis=0)


def window_mask(block_lists, counts, head_ids, base, blocks):
    span = 2 * MARGIN + 1
    list_length = block_lists.shape[2]
    head_lists = jnp.take(block_lists, head_ids, axis=0)
    head_counts = jnp.take(counts, head_ids, axis=0)
    global_ids = base[:, None] + jnp.arange(blocks, dtype=jnp.int32)[None, :]
    lists = jnp.take_along_axis(head_lists, global_ids[:, :, None], axis=1)
    used = jnp.take_along_axis(head_counts, global_ids, axis=1)
    wanted = global_ids[:, :, None] + jnp.arange(span, dtype=jnp.int32)[None, None, :] - MARGIN
    live = jnp.arange(list_length, dtype=jnp.int32)[None, None, :] < used[:, :, None]
    hit = (lists[:, :, None, :] == wanted[:, :, :, None]) & live[:, :, None, :]
    return jnp.any(hit, axis=-1)


def attend(query_rows, key_ext, value_ext, allowed, logit_scale, value_factor):
    rows, heads, width = query_rows.shape
    blocks = rows // BLOCK
    span = 2 * MARGIN + 1
    q = query_rows.reshape(blocks, BLOCK, heads, width)
    kb = key_ext.reshape(blocks + 2 * MARGIN, BLOCK, heads, width)
    vb = value_ext.reshape(blocks + 2 * MARGIN, BLOCK, heads, width)
    kw = jnp.stack([kb[o : o + blocks] for o in range(span)], axis=1)
    vw = jnp.stack([vb[o : o + blocks] for o in range(span)], axis=1)
    logits = jnp.einsum("bqhd,bokhd->hbqok", q, kw, preferred_element_type=jnp.float32)
    logits = logits * logit_scale[:, None, None, None, None]
    logits = jnp.where(allowed[:, :, None, :, None], logits, -jnp.inf)
    peak = jnp.max(logits, axis=(3, 4), keepdims=True)
    weight = jnp.exp(logits - peak)
    total = jnp.sum(weight, axis=(3, 4))
    mixed = jnp.einsum(
        "hbqok,bokhd->bqhd", weight.astype(jnp.bfloat16), vw, preferred_element_type=jnp.float32
    )
    factor = value_factor[:, None, None] / total
    out = mixed * jnp.transpose(factor, (1, 2, 0))[:, :, :, None]
    return out.astype(jnp.bfloat16).reshape(rows, heads, width)


def shards(
    queries,
    key_vectors,
    value_vectors,
    labels,
    block_lists,
    counts,
    query_scale,
    key_scale,
    value_scale,
):
    groups = lax.axis_size("ulysses")
    frames = lax.axis_size("frame")
    quarters = lax.axis_size("quarter")
    devices_along = frames * quarters
    tokens_here = queries.shape[0]
    head_count = labels.shape[0]
    width = queries.shape[1] // head_count
    per_group = head_count // groups
    rows = tokens_here * groups
    blocks = rows // BLOCK
    piece = rows // frames

    group_index = lax.axis_index("ulysses")
    frame_index = lax.axis_index("frame")
    quarter_index = lax.axis_index("quarter")
    spatial_slot = frame_index * quarters + quarter_index
    temporal_slot = quarter_index * frames + frame_index

    stacked = jnp.concatenate(
        [
            queries.reshape(tokens_here, groups, per_group, width),
            key_vectors.reshape(tokens_here, groups, per_group, width),
            value_vectors.reshape(tokens_here, groups, per_group, width),
        ],
        axis=2,
    )
    frame_rows = lax.all_to_all(stacked, "ulysses", split_axis=1, concat_axis=0, tiled=True)
    frame_rows = frame_rows.reshape(rows, 3 * per_group, width)
    moved = lax.all_to_all(
        frame_rows.reshape(frames, piece, 3 * per_group, width),
        "frame",
        split_axis=0,
        concat_axis=0,
        tiled=True,
    )
    line_rows = jnp.transpose(moved, (1, 0, 2, 3)).reshape(rows, 3 * per_group, width)

    spatial_order = list(range(devices_along))
    temporal_order = [(k % frames) * quarters + k // frames for k in range(devices_along)]
    frame_ext = with_halo(frame_rows[:, per_group:], ("frame", "quarter"), spatial_order)
    line_ext = with_halo(line_rows[:, per_group:], ("frame", "quarter"), temporal_order)

    head_ids = group_index * per_group + jnp.arange(per_group, dtype=jnp.int32)
    temporal = jnp.take(labels, head_ids) == 1
    doubled = jnp.concatenate([temporal, temporal])
    query_rows = jnp.where(temporal[None, :, None], line_rows[:, :per_group], frame_rows[:, :per_group])
    extended = jnp.where(doubled[None, :, None], line_ext, frame_ext)
    base = jnp.where(temporal, temporal_slot * blocks, spatial_slot * blocks).astype(jnp.int32)
    allowed = window_mask(block_lists, counts, head_ids, base, blocks)
    logit_scale = (
        jnp.take(query_scale, head_ids) * jnp.take(key_scale, head_ids) / math.sqrt(width)
    )
    value_factor = jnp.take(value_scale, head_ids)
    outputs = attend(
        query_rows,
        extended[:, :per_group],
        extended[:, per_group:],
        allowed,
        logit_scale,
        value_factor,
    )

    back = jnp.transpose(outputs.reshape(piece, frames, per_group, width), (1, 0, 2, 3))
    returned = lax.all_to_all(back, "frame", split_axis=0, concat_axis=0, tiled=True)
    returned = returned.reshape(rows, per_group, width)
    frame_outputs = jnp.where(temporal[None, :, None], returned, outputs)
    merged = lax.all_to_all(
        frame_outputs.reshape(rows, 1, per_group, width),
        "ulysses",
        split_axis=0,
        concat_axis=1,
        tiled=True,
    )
    return merged.reshape(tokens_here, head_count * width)


def solution(mesh):
    ulysses, context = mesh.devices.shape
    fine = Mesh(
        mesh.devices.reshape(ulysses, FRAMES, context // FRAMES), ("ulysses", "frame", "quarter")
    )
    rows = P(("frame", "quarter", "ulysses"), None)
    placed = (rows, rows, rows, P(), P(), P(), P(), P(), P())
    return jax.shard_map(
        shards,
        mesh=fine,
        in_specs=placed,
        out_specs=rows,
        check_vma=False,
    )
```

```python
import math

import jax
import jax.numpy as jnp
from jax import lax
from jax.sharding import Mesh, PartitionSpec as P

FRAMES = 16
MARGIN = 2
BLOCK = 64
TEMPORAL = 16


def with_halo(cells, axes, order):
    width = MARGIN * BLOCK
    pairs = list(zip(order[:-1], order[1:]))
    lower = lax.ppermute(cells[-width:], axes, pairs)
    upper = lax.ppermute(cells[:width], axes, [(b, a) for a, b in pairs])
    return jnp.concatenate([lower, cells, upper], axis=0)


def window_mask(block_lists, counts, head_ids, base, blocks):
    span = 2 * MARGIN + 1
    list_length = block_lists.shape[2]
    head_lists = jnp.take(block_lists, head_ids, axis=0)
    head_counts = jnp.take(counts, head_ids, axis=0)
    global_ids = base[:, None] + jnp.arange(blocks, dtype=jnp.int32)[None, :]
    lists = jnp.take_along_axis(head_lists, global_ids[:, :, None], axis=1)
    used = jnp.take_along_axis(head_counts, global_ids, axis=1)
    wanted = global_ids[:, :, None] + jnp.arange(span, dtype=jnp.int32)[None, None, :] - MARGIN
    live = jnp.arange(list_length, dtype=jnp.int32)[None, None, :] < used[:, :, None]
    hit = (lists[:, :, None, :] == wanted[:, :, :, None]) & live[:, :, None, :]
    return jnp.any(hit, axis=-1)


def attend(query_rows, key_ext, value_ext, allowed, logit_scale, value_factor):
    rows, heads, width = query_rows.shape
    blocks = rows // BLOCK
    span = 2 * MARGIN + 1
    q = query_rows.reshape(blocks, BLOCK, heads, width)
    kb = key_ext.reshape(blocks + 2 * MARGIN, BLOCK, heads, width)
    vb = value_ext.reshape(blocks + 2 * MARGIN, BLOCK, heads, width)
    kw = jnp.stack([kb[o : o + blocks] for o in range(span)], axis=1)
    vw = jnp.stack([vb[o : o + blocks] for o in range(span)], axis=1)
    logits = jnp.einsum("bqhd,bokhd->hbqok", q, kw, preferred_element_type=jnp.float32)
    logits = logits * logit_scale[:, None, None, None, None]
    logits = jnp.where(allowed[:, :, None, :, None], logits, -jnp.inf)
    peak = jnp.max(logits, axis=(3, 4), keepdims=True)
    weight = jnp.exp(logits - peak)
    total = jnp.sum(weight, axis=(3, 4))
    mixed = jnp.einsum(
        "hbqok,bokhd->bqhd", weight.astype(jnp.bfloat16), vw, preferred_element_type=jnp.float32
    )
    factor = value_factor[:, None, None] / total
    out = mixed * jnp.transpose(factor, (1, 2, 0))[:, :, :, None]
    return out.astype(jnp.bfloat16).reshape(rows, heads, width)


def shards(
    queries,
    key_vectors,
    value_vectors,
    labels,
    block_lists,
    counts,
    query_scale,
    key_scale,
    value_scale,
):
    groups = lax.axis_size("ulysses")
    frames = lax.axis_size("frame")
    quarters = lax.axis_size("quarter")
    devices_along = frames * quarters
    tokens_here = queries.shape[0]
    head_count = labels.shape[0]
    width = queries.shape[1] // head_count
    per_group = head_count // groups
    lines_per_group = TEMPORAL // groups
    spaces_per_group = per_group - lines_per_group
    rows = tokens_here * groups
    blocks = rows // BLOCK
    piece = rows // frames

    group_index = lax.axis_index("ulysses")
    frame_index = lax.axis_index("frame")
    quarter_index = lax.axis_index("quarter")
    spatial_slot = frame_index * quarters + quarter_index
    temporal_slot = quarter_index * frames + frame_index

    ranked = jnp.argsort(1 - labels, stable=True).astype(jnp.int32)
    slots = jnp.concatenate(
        [
            ranked[:TEMPORAL].reshape(groups, lines_per_group),
            ranked[TEMPORAL:].reshape(groups, spaces_per_group),
        ],
        axis=1,
    ).reshape(head_count)
    unslots = jnp.argsort(slots).astype(jnp.int32)

    def grouped(array):
        picked = jnp.take(array.reshape(tokens_here, head_count, width), slots, axis=1)
        return picked.reshape(tokens_here, groups, per_group, width)

    gq, gk, gv = grouped(queries), grouped(key_vectors), grouped(value_vectors)
    lo, hi = slice(0, lines_per_group), slice(lines_per_group, per_group)
    stacked = jnp.concatenate(
        [gq[:, :, lo], gk[:, :, lo], gv[:, :, lo], gq[:, :, hi], gk[:, :, hi], gv[:, :, hi]], axis=2
    )
    frame_rows = lax.all_to_all(stacked, "ulysses", split_axis=1, concat_axis=0, tiled=True)
    frame_rows = frame_rows.reshape(rows, 3 * per_group, width)
    line_part = frame_rows[:, : 3 * lines_per_group]
    space_part = frame_rows[:, 3 * lines_per_group :]
    moved = lax.all_to_all(
        line_part.reshape(frames, piece, 3 * lines_per_group, width),
        "frame",
        split_axis=0,
        concat_axis=0,
        tiled=True,
    )
    line_rows = jnp.transpose(moved, (1, 0, 2, 3)).reshape(rows, 3 * lines_per_group, width)

    spatial_order = list(range(devices_along))
    temporal_order = [(k % frames) * quarters + k // frames for k in range(devices_along)]
    space_ext = with_halo(space_part[:, spaces_per_group:], ("frame", "quarter"), spatial_order)
    line_ext = with_halo(line_rows[:, lines_per_group:], ("frame", "quarter"), temporal_order)

    group_heads = lax.dynamic_slice_in_dim(slots, group_index * per_group, per_group)
    logit_scale = (
        jnp.take(query_scale, group_heads) * jnp.take(key_scale, group_heads) / math.sqrt(width)
    )
    value_factor = jnp.take(value_scale, group_heads)

    def run(part_rows, ext, heads, base):
        n = heads.stop - heads.start
        ids = group_heads[heads]
        allowed = window_mask(
            block_lists, counts, ids, jnp.full((n,), base * blocks, jnp.int32), blocks
        )
        return attend(
            part_rows[:, :n], ext[:, :n], ext[:, n:], allowed, logit_scale[heads], value_factor[heads]
        )

    line_out = run(line_rows, line_ext, lo, temporal_slot)
    space_out = run(space_part, space_ext, hi, spatial_slot)

    back = jnp.transpose(line_out.reshape(piece, frames, lines_per_group, width), (1, 0, 2, 3))
    returned = lax.all_to_all(back, "frame", split_axis=0, concat_axis=0, tiled=True)
    returned = returned.reshape(rows, lines_per_group, width)
    frame_outputs = jnp.concatenate([returned, space_out], axis=1)
    merged = lax.all_to_all(
        frame_outputs.reshape(rows, 1, per_group, width),
        "ulysses",
        split_axis=0,
        concat_axis=1,
        tiled=True,
    )
    merged = jnp.take(merged.reshape(tokens_here, head_count, width), unslots, axis=1)
    return merged.reshape(tokens_here, head_count * width)


def solution(mesh):
    ulysses, context = mesh.devices.shape
    fine = Mesh(
        mesh.devices.reshape(ulysses, FRAMES, context // FRAMES), ("ulysses", "frame", "quarter")
    )
    rows = P(("frame", "quarter", "ulysses"), None)
    placed = (rows, rows, rows, P(), P(), P(), P(), P(), P())
    return jax.shard_map(
        shards,
        mesh=fine,
        in_specs=placed,
        out_specs=rows,
        check_vma=False,
    )
```

```python
import math

import jax
import jax.numpy as jnp
from jax import lax
from jax.sharding import Mesh, PartitionSpec as P

FRAMES = 16
MARGIN = 2
BLOCK = 64
TEMPORAL = 16
HEAD_SPLIT = 4


def with_halo(cells, axes, order):
    width = MARGIN * BLOCK
    pairs = list(zip(order[:-1], order[1:]))
    lower = lax.ppermute(cells[-width:], axes, pairs)
    upper = lax.ppermute(cells[:width], axes, [(b, a) for a, b in pairs])
    return jnp.concatenate([lower, cells, upper], axis=0)


def window_mask(block_lists, counts, head_ids, base, blocks):
    span = 2 * MARGIN + 1
    list_length = block_lists.shape[2]
    head_lists = jnp.take(block_lists, head_ids, axis=0)
    head_counts = jnp.take(counts, head_ids, axis=0)
    global_ids = base[:, None] + jnp.arange(blocks, dtype=jnp.int32)[None, :]
    lists = jnp.take_along_axis(head_lists, global_ids[:, :, None], axis=1)
    used = jnp.take_along_axis(head_counts, global_ids, axis=1)
    wanted = global_ids[:, :, None] + jnp.arange(span, dtype=jnp.int32)[None, None, :] - MARGIN
    live = jnp.arange(list_length, dtype=jnp.int32)[None, None, :] < used[:, :, None]
    hit = (lists[:, :, None, :] == wanted[:, :, :, None]) & live[:, :, None, :]
    return jnp.any(hit, axis=-1)


def attend(query_rows, key_ext, value_ext, allowed, logit_scale, value_factor):
    rows, heads, width = query_rows.shape
    blocks = rows // BLOCK
    span = 2 * MARGIN + 1
    q = query_rows.reshape(blocks, BLOCK, heads, width)
    kb = key_ext.reshape(blocks + 2 * MARGIN, BLOCK, heads, width)
    vb = value_ext.reshape(blocks + 2 * MARGIN, BLOCK, heads, width)
    kw = jnp.stack([kb[o : o + blocks] for o in range(span)], axis=1)
    vw = jnp.stack([vb[o : o + blocks] for o in range(span)], axis=1)
    logits = jnp.einsum("bqhd,bokhd->hbqok", q, kw, preferred_element_type=jnp.float32)
    logits = logits * logit_scale[:, None, None, None, None]
    logits = jnp.where(allowed[:, :, None, :, None], logits, -jnp.inf)
    peak = jnp.max(logits, axis=(3, 4), keepdims=True)
    weight = jnp.exp(logits - peak)
    total = jnp.sum(weight, axis=(3, 4))
    mixed = jnp.einsum(
        "hbqok,bokhd->bqhd", weight.astype(jnp.bfloat16), vw, preferred_element_type=jnp.float32
    )
    factor = value_factor[:, None, None] / total
    out = mixed * jnp.transpose(factor, (1, 2, 0))[:, :, :, None]
    return out.astype(jnp.bfloat16).reshape(rows, heads, width)


def shards(
    queries,
    key_vectors,
    value_vectors,
    labels,
    block_lists,
    counts,
    query_scale,
    key_scale,
    value_scale,
):
    groups = lax.axis_size("x")
    halves = lax.axis_size("zh")
    frames = lax.axis_size("frame")
    quarters = lax.axis_size("quarter")
    tokens_here = queries.shape[0]
    head_count = labels.shape[0]
    width = queries.shape[1] // head_count
    per_group = head_count // groups
    lines_per_group = TEMPORAL // groups
    spaces_per_group = per_group - lines_per_group
    rows = tokens_here * groups
    blocks = rows // BLOCK
    piece = rows // frames
    chunks = frames * quarters * halves

    group_index = lax.axis_index("x")
    half_index = lax.axis_index("zh")
    frame_index = lax.axis_index("frame")
    quarter_index = lax.axis_index("quarter")
    spatial_slot = (frame_index * quarters + quarter_index) * halves + half_index
    temporal_slot = (quarter_index * halves + half_index) * frames + frame_index

    ranked = jnp.argsort(1 - labels, stable=True).astype(jnp.int32)
    slots = jnp.concatenate(
        [
            ranked[:TEMPORAL].reshape(groups, lines_per_group),
            ranked[TEMPORAL:].reshape(groups, spaces_per_group),
        ],
        axis=1,
    ).reshape(head_count)
    unslots = jnp.argsort(slots).astype(jnp.int32)

    def grouped(array):
        picked = jnp.take(array.reshape(tokens_here, head_count, width), slots, axis=1)
        return picked.reshape(tokens_here, groups, per_group, width)

    gq, gk, gv = grouped(queries), grouped(key_vectors), grouped(value_vectors)
    lo, hi = slice(0, lines_per_group), slice(lines_per_group, per_group)
    stacked = jnp.concatenate(
        [gq[:, :, lo], gk[:, :, lo], gv[:, :, lo], gq[:, :, hi], gk[:, :, hi], gv[:, :, hi]], axis=2
    )
    frame_rows = lax.all_to_all(stacked, "x", split_axis=1, concat_axis=0, tiled=True)
    frame_rows = frame_rows.reshape(rows, 3 * per_group, width)
    line_part = frame_rows[:, : 3 * lines_per_group]
    space_part = frame_rows[:, 3 * lines_per_group :]
    moved = lax.all_to_all(
        line_part.reshape(frames, piece, 3 * lines_per_group, width),
        "frame",
        split_axis=0,
        concat_axis=0,
        tiled=True,
    )
    line_rows = jnp.transpose(moved, (1, 0, 2, 3)).reshape(rows, 3 * lines_per_group, width)

    def linear(half, frame, quarter):
        return (half * frames + frame) * quarters + quarter

    spatial_order = [
        linear(k % halves, k // (halves * quarters), (k // halves) % quarters) for k in range(chunks)
    ]
    temporal_order = [
        linear((k // frames) % halves, k % frames, k // (frames * halves)) for k in range(chunks)
    ]
    along = ("zh", "frame", "quarter")
    space_ext = with_halo(space_part[:, spaces_per_group:], along, spatial_order)
    line_ext = with_halo(line_rows[:, lines_per_group:], along, temporal_order)

    group_heads = lax.dynamic_slice_in_dim(slots, group_index * per_group, per_group)
    logit_scale = (
        jnp.take(query_scale, group_heads) * jnp.take(key_scale, group_heads) / math.sqrt(width)
    )
    value_factor = jnp.take(value_scale, group_heads)

    def run(part_rows, ext, heads, base):
        n = heads.stop - heads.start
        ids = group_heads[heads]
        allowed = window_mask(
            block_lists, counts, ids, jnp.full((n,), base * blocks, jnp.int32), blocks
        )
        return attend(
            part_rows[:, :n], ext[:, :n], ext[:, n:], allowed, logit_scale[heads], value_factor[heads]
        )

    line_out = run(line_rows, line_ext, lo, temporal_slot)
    space_out = run(space_part, space_ext, hi, spatial_slot)

    back = jnp.transpose(line_out.reshape(piece, frames, lines_per_group, width), (1, 0, 2, 3))
    returned = lax.all_to_all(back, "frame", split_axis=0, concat_axis=0, tiled=True)
    returned = returned.reshape(rows, lines_per_group, width)
    frame_outputs = jnp.concatenate([returned, space_out], axis=1)
    merged = lax.all_to_all(
        frame_outputs.reshape(rows, 1, per_group, width),
        "x",
        split_axis=0,
        concat_axis=1,
        tiled=True,
    )
    merged = jnp.take(merged.reshape(tokens_here, head_count, width), unslots, axis=1)
    return merged.reshape(tokens_here, head_count * width)


def solution(mesh):
    ulysses, context = mesh.devices.shape
    halves = mesh.devices.size // (context * HEAD_SPLIT)
    fine = Mesh(
        mesh.devices.reshape(halves, HEAD_SPLIT, FRAMES, context // FRAMES),
        ("zh", "x", "frame", "quarter"),
    )
    rows = P(("frame", "quarter", "zh", "x"), None)
    placed = (rows, rows, rows, P(), P(), P(), P(), P(), P())
    return jax.shard_map(
        shards,
        mesh=fine,
        in_specs=placed,
        out_specs=rows,
        check_vma=False,
    )
```

```python
import math

import jax
import jax.numpy as jnp
from jax import lax
from jax.sharding import Mesh, PartitionSpec as P

FRAMES = 16
MARGIN = 2
BLOCK = 64
TEMPORAL = 16
HEAD_SPLIT = 4


def with_halo(cells, axes, order):
    width = MARGIN * BLOCK
    pairs = list(zip(order[:-1], order[1:]))
    lower = lax.ppermute(cells[-width:], axes, pairs)
    upper = lax.ppermute(cells[:width], axes, [(b, a) for a, b in pairs])
    return jnp.concatenate([lower, cells, upper], axis=0)


def window_mask(block_lists, counts, head_ids, base, blocks):
    span = 2 * MARGIN + 1
    list_length = block_lists.shape[2]
    head_lists = jnp.take(block_lists, head_ids, axis=0)
    head_counts = jnp.take(counts, head_ids, axis=0)
    global_ids = base[:, None] + jnp.arange(blocks, dtype=jnp.int32)[None, :]
    lists = jnp.take_along_axis(head_lists, global_ids[:, :, None], axis=1)
    used = jnp.take_along_axis(head_counts, global_ids, axis=1)
    wanted = global_ids[:, :, None] + jnp.arange(span, dtype=jnp.int32)[None, None, :] - MARGIN
    live = jnp.arange(list_length, dtype=jnp.int32)[None, None, :] < used[:, :, None]
    hit = (lists[:, :, None, :] == wanted[:, :, :, None]) & live[:, :, None, :]
    return jnp.any(hit, axis=-1)


def attend(query_rows, key_ext, value_ext, allowed, logit_scale, value_factor):
    rows, heads, width = query_rows.shape
    blocks = rows // BLOCK
    span = 2 * MARGIN + 1
    q = query_rows.reshape(blocks, BLOCK, heads, width)
    kb = key_ext.reshape(blocks + 2 * MARGIN, BLOCK, heads, width)
    vb = value_ext.reshape(blocks + 2 * MARGIN, BLOCK, heads, width)
    kw = jnp.stack([kb[o : o + blocks] for o in range(span)], axis=1)
    vw = jnp.stack([vb[o : o + blocks] for o in range(span)], axis=1)
    logits = jnp.einsum("bqhd,bokhd->hbqok", q, kw, preferred_element_type=jnp.float32)
    logits = logits * logit_scale[:, None, None, None, None]
    logits = jnp.where(allowed[:, :, None, :, None], logits, -jnp.inf)
    peak = jnp.max(logits, axis=(3, 4), keepdims=True)
    weight = jnp.exp(logits - peak)
    total = jnp.sum(weight, axis=(3, 4))
    mixed = jnp.einsum(
        "hbqok,bokhd->bqhd", weight.astype(jnp.bfloat16), vw, preferred_element_type=jnp.float32
    )
    factor = value_factor[:, None, None] / total
    out = mixed * jnp.transpose(factor, (1, 2, 0))[:, :, :, None]
    return out.astype(jnp.bfloat16).reshape(rows, heads, width)


def shards(
    queries,
    key_vectors,
    value_vectors,
    labels,
    block_lists,
    counts,
    query_scale,
    key_scale,
    value_scale,
):
    groups = lax.axis_size("x")
    halves = lax.axis_size("zh")
    frames = lax.axis_size("frame")
    quarters = lax.axis_size("quarter")
    tokens_here = queries.shape[0]
    head_count = labels.shape[0]
    width = queries.shape[1] // head_count
    per_group = head_count // groups
    lines_per_group = TEMPORAL // groups
    spaces_per_group = per_group - lines_per_group
    rows = tokens_here * groups
    blocks = rows // BLOCK
    piece = rows // frames
    chunks = frames * quarters * halves

    group_index = lax.axis_index("x")
    half_index = lax.axis_index("zh")
    frame_index = lax.axis_index("frame")
    quarter_index = lax.axis_index("quarter")
    spatial_slot = (frame_index * quarters + quarter_index) * halves + half_index

    ranked = jnp.argsort(1 - labels, stable=True).astype(jnp.int32)
    slots = jnp.concatenate(
        [
            ranked[:TEMPORAL].reshape(groups, lines_per_group),
            ranked[TEMPORAL:].reshape(groups, spaces_per_group),
        ],
        axis=1,
    ).reshape(head_count)
    unslots = jnp.argsort(slots).astype(jnp.int32)

    def grouped(array):
        picked = jnp.take(array.reshape(tokens_here, head_count, width), slots, axis=1)
        return picked.reshape(tokens_here, groups, per_group, width)

    gq, gk, gv = grouped(queries), grouped(key_vectors), grouped(value_vectors)
    lo, hi = slice(0, lines_per_group), slice(lines_per_group, per_group)
    stacked = jnp.concatenate(
        [gq[:, :, lo], gk[:, :, lo], gv[:, :, lo], gq[:, :, hi], gk[:, :, hi], gv[:, :, hi]], axis=2
    )
    frame_rows = lax.all_to_all(stacked, "x", split_axis=1, concat_axis=0, tiled=True)
    frame_rows = frame_rows.reshape(rows, 3 * per_group, width)
    line_part = frame_rows[:, : 3 * lines_per_group]
    space_part = frame_rows[:, 3 * lines_per_group :]
    piece_of = [j // 2 if j % 2 == 0 else frames - 1 - j // 2 for j in range(frames)]
    holder_of = [piece_of.index(k) for k in range(frames)]
    pieces = line_part.reshape(frames, piece, 3 * lines_per_group, width)
    moved = lax.all_to_all(
        jnp.stack([pieces[k] for k in piece_of]),
        "frame",
        split_axis=0,
        concat_axis=0,
        tiled=True,
    )
    space_kv = space_part[:, spaces_per_group:]
    moved, space_kv = lax.optimization_barrier((moved, space_kv))
    line_rows = jnp.transpose(moved, (1, 0, 2, 3)).reshape(rows, 3 * lines_per_group, width)

    def linear(half, frame, quarter):
        return (half * frames + frame) * quarters + quarter

    spatial_order = [
        linear(k % halves, k // (halves * quarters), (k // halves) % quarters) for k in range(chunks)
    ]
    temporal_order = [
        linear((k // frames) % halves, holder_of[k % frames], k // (frames * halves))
        for k in range(chunks)
    ]
    along = ("zh", "frame", "quarter")
    space_ext = with_halo(space_kv, along, spatial_order)
    line_ext = with_halo(line_rows[:, lines_per_group:], along, temporal_order)

    group_heads = lax.dynamic_slice_in_dim(slots, group_index * per_group, per_group)
    logit_scale = (
        jnp.take(query_scale, group_heads) * jnp.take(key_scale, group_heads) / math.sqrt(width)
    )
    value_factor = jnp.take(value_scale, group_heads)

    def run(part_rows, ext, heads, base):
        n = heads.stop - heads.start
        ids = group_heads[heads]
        allowed = window_mask(
            block_lists, counts, ids, jnp.full((n,), base * blocks, jnp.int32), blocks
        )
        return attend(
            part_rows[:, :n], ext[:, :n], ext[:, n:], allowed, logit_scale[heads], value_factor[heads]
        )

    own_piece = jnp.asarray(piece_of, jnp.int32)[frame_index]
    temporal_slot = (quarter_index * halves + half_index) * frames + own_piece
    line_out = run(line_rows, line_ext, lo, temporal_slot)
    space_out = run(space_part, space_ext, hi, spatial_slot)

    back = jnp.transpose(line_out.reshape(piece, frames, lines_per_group, width), (1, 0, 2, 3))
    returned = lax.all_to_all(back, "frame", split_axis=0, concat_axis=0, tiled=True)
    returned = jnp.stack([returned[j] for j in holder_of]).reshape(rows, lines_per_group, width)
    frame_outputs = jnp.concatenate([returned, space_out], axis=1)
    merged = lax.all_to_all(
        frame_outputs.reshape(rows, 1, per_group, width),
        "x",
        split_axis=0,
        concat_axis=1,
        tiled=True,
    )
    merged = jnp.take(merged.reshape(tokens_here, head_count, width), unslots, axis=1)
    return merged.reshape(tokens_here, head_count * width)


def solution(mesh):
    ulysses, context = mesh.devices.shape
    halves = mesh.devices.size // (context * HEAD_SPLIT)
    fine = Mesh(
        mesh.devices.reshape(halves, HEAD_SPLIT, FRAMES, context // FRAMES),
        ("zh", "x", "frame", "quarter"),
    )
    rows = P(("frame", "quarter", "zh", "x"), None)
    placed = (rows, rows, rows, P(), P(), P(), P(), P(), P())
    return jax.shard_map(
        shards,
        mesh=fine,
        in_specs=placed,
        out_specs=rows,
        check_vma=False,
    )
```

```python
import math

import jax
import jax.numpy as jnp
from jax import lax
from jax.sharding import Mesh, PartitionSpec as P

FRAMES = 16
MARGIN = 2
BLOCK = 64
TEMPORAL = 16
HEAD_SPLIT = 4


def with_halo(cells, axes, order):
    width = MARGIN * BLOCK
    pairs = list(zip(order[:-1], order[1:]))
    lower = lax.ppermute(cells[-width:], axes, pairs)
    upper = lax.ppermute(cells[:width], axes, [(b, a) for a, b in pairs])
    return jnp.concatenate([lower, cells, upper], axis=0)


def window_mask(block_lists, counts, head_ids, base, blocks):
    span = 2 * MARGIN + 1
    list_length = block_lists.shape[2]
    head_lists = jnp.take(block_lists, head_ids, axis=0)
    head_counts = jnp.take(counts, head_ids, axis=0)
    global_ids = base[:, None] + jnp.arange(blocks, dtype=jnp.int32)[None, :]
    lists = jnp.take_along_axis(head_lists, global_ids[:, :, None], axis=1)
    used = jnp.take_along_axis(head_counts, global_ids, axis=1)
    wanted = global_ids[:, :, None] + jnp.arange(span, dtype=jnp.int32)[None, None, :] - MARGIN
    live = jnp.arange(list_length, dtype=jnp.int32)[None, None, :] < used[:, :, None]
    hit = (lists[:, :, None, :] == wanted[:, :, :, None]) & live[:, :, None, :]
    return jnp.any(hit, axis=-1)


def attend(query_rows, key_ext, value_ext, allowed, logit_scale, value_factor):
    rows, heads, width = query_rows.shape
    blocks = rows // BLOCK
    span = 2 * MARGIN + 1
    q = query_rows.reshape(blocks, BLOCK, heads, width)
    kb = key_ext.reshape(blocks + 2 * MARGIN, BLOCK, heads, width)
    vb = value_ext.reshape(blocks + 2 * MARGIN, BLOCK, heads, width)
    kw = jnp.stack([kb[o : o + blocks] for o in range(span)], axis=1)
    vw = jnp.stack([vb[o : o + blocks] for o in range(span)], axis=1)
    logits = jnp.einsum("bqhd,bokhd->hbqok", q, kw, preferred_element_type=jnp.float32)
    logits = logits * logit_scale[:, None, None, None, None]
    logits = jnp.where(allowed[:, :, None, :, None], logits, -jnp.inf)
    peak = jnp.max(logits, axis=(3, 4), keepdims=True)
    weight = jnp.exp(logits - peak)
    total = jnp.sum(weight, axis=(3, 4))
    mixed = jnp.einsum(
        "hbqok,bokhd->bqhd", weight.astype(jnp.bfloat16), vw, preferred_element_type=jnp.float32
    )
    factor = value_factor[:, None, None] / total
    out = mixed * jnp.transpose(factor, (1, 2, 0))[:, :, :, None]
    return out.astype(jnp.bfloat16).reshape(rows, heads, width)


def shards(
    queries,
    key_vectors,
    value_vectors,
    labels,
    block_lists,
    counts,
    query_scale,
    key_scale,
    value_scale,
):
    groups = lax.axis_size("x")
    halves = lax.axis_size("zh")
    frames = lax.axis_size("frame")
    quarters = lax.axis_size("quarter")
    tokens_here = queries.shape[0]
    head_count = labels.shape[0]
    width = queries.shape[1] // head_count
    per_group = head_count // groups
    lines_per_group = TEMPORAL // groups
    spaces_per_group = per_group - lines_per_group
    rows = tokens_here * groups
    blocks = rows // BLOCK
    piece = rows // frames
    chunks = frames * quarters * halves

    group_index = lax.axis_index("x")
    half_index = lax.axis_index("zh")
    frame_index = lax.axis_index("frame")
    quarter_index = lax.axis_index("quarter")
    spatial_slot = (frame_index * quarters + quarter_index) * halves + half_index
    temporal_slot = (quarter_index * halves + half_index) * frames + frame_index

    heads = jnp.arange(head_count, dtype=jnp.int32)
    earlier = heads[None, :] < heads[:, None]
    is_line = labels == 1
    line_rank = jnp.sum(jnp.where(earlier, is_line[None, :], False), axis=1, dtype=jnp.int32)
    space_rank = heads - line_rank
    unslots = jnp.where(
        is_line,
        (line_rank // lines_per_group) * per_group + line_rank % lines_per_group,
        (space_rank // spaces_per_group) * per_group + lines_per_group + space_rank % spaces_per_group,
    )
    slots = jnp.sum(jnp.where(unslots[None, :] == heads[:, None], heads[None, :], 0), axis=1)

    def grouped(array):
        picked = jnp.take(array.reshape(tokens_here, head_count, width), slots, axis=1)
        return picked.reshape(tokens_here, groups, per_group, width)

    gq, gk, gv = grouped(queries), grouped(key_vectors), grouped(value_vectors)
    lo, hi = slice(0, lines_per_group), slice(lines_per_group, per_group)
    stacked = jnp.concatenate(
        [gq[:, :, lo], gk[:, :, lo], gv[:, :, lo], gq[:, :, hi], gk[:, :, hi], gv[:, :, hi]], axis=2
    )
    frame_rows = lax.all_to_all(stacked, "x", split_axis=1, concat_axis=0, tiled=True)
    frame_rows = frame_rows.reshape(rows, 3 * per_group, width)
    line_part = frame_rows[:, : 3 * lines_per_group]
    space_part = frame_rows[:, 3 * lines_per_group :]
    moved = lax.all_to_all(
        line_part.reshape(frames, piece, 3 * lines_per_group, width),
        "frame",
        split_axis=0,
        concat_axis=0,
        tiled=True,
    )
    space_kv = space_part[:, spaces_per_group:]
    moved, space_kv = lax.optimization_barrier((moved, space_kv))
    line_rows = jnp.transpose(moved, (1, 0, 2, 3)).reshape(rows, 3 * lines_per_group, width)

    def linear(half, frame, quarter):
        return (half * frames + frame) * quarters + quarter

    spatial_order = [
        linear(k % halves, k // (halves * quarters), (k // halves) % quarters) for k in range(chunks)
    ]
    temporal_order = [
        linear((k // frames) % halves, k % frames, k // (frames * halves)) for k in range(chunks)
    ]
    along = ("zh", "frame", "quarter")
    space_ext = with_halo(space_kv, along, spatial_order)
    line_ext = with_halo(line_rows[:, lines_per_group:], along, temporal_order)

    group_heads = lax.dynamic_slice_in_dim(slots, group_index * per_group, per_group)
    logit_scale = (
        jnp.take(query_scale, group_heads) * jnp.take(key_scale, group_heads) / math.sqrt(width)
    )
    value_factor = jnp.take(value_scale, group_heads)

    def run(part_rows, ext, heads, base):
        n = heads.stop - heads.start
        ids = group_heads[heads]
        allowed = window_mask(
            block_lists, counts, ids, jnp.full((n,), base * blocks, jnp.int32), blocks
        )
        return attend(
            part_rows[:, :n], ext[:, :n], ext[:, n:], allowed, logit_scale[heads], value_factor[heads]
        )

    line_out = run(line_rows, line_ext, lo, temporal_slot)
    back = jnp.transpose(line_out.reshape(piece, frames, lines_per_group, width), (1, 0, 2, 3))
    back, space_ext = lax.optimization_barrier((back, space_ext))
    space_out = run(space_part, space_ext, hi, spatial_slot)

    returned = lax.all_to_all(back, "frame", split_axis=0, concat_axis=0, tiled=True)
    returned = returned.reshape(rows, lines_per_group, width)
    frame_outputs = jnp.concatenate([returned, space_out], axis=1)
    merged = lax.all_to_all(
        frame_outputs.reshape(rows, 1, per_group, width),
        "x",
        split_axis=0,
        concat_axis=1,
        tiled=True,
    )
    merged = jnp.take(merged.reshape(tokens_here, head_count, width), unslots, axis=1)
    return merged.reshape(tokens_here, head_count * width)


def solution(mesh):
    ulysses, context = mesh.devices.shape
    halves = mesh.devices.size // (context * HEAD_SPLIT)
    fine = Mesh(
        mesh.devices.reshape(halves, HEAD_SPLIT, FRAMES, context // FRAMES),
        ("zh", "x", "frame", "quarter"),
    )
    rows = P(("frame", "quarter", "zh", "x"), None)
    placed = (rows, rows, rows, P(), P(), P(), P(), P(), P())
    return jax.shard_map(
        shards,
        mesh=fine,
        in_specs=placed,
        out_specs=rows,
        check_vma=False,
    )
```

```python
import math

import jax
import jax.numpy as jnp
from jax import lax
from jax.sharding import Mesh, PartitionSpec as P

FRAMES = 16
MARGIN = 2
BLOCK = 64
TEMPORAL = 16
HEAD_SPLIT = 4


def with_halo(cells, axes, order):
    width = MARGIN * BLOCK
    pairs = list(zip(order[:-1], order[1:]))
    lower = lax.ppermute(cells[-width:], axes, pairs)
    upper = lax.ppermute(cells[:width], axes, [(b, a) for a, b in pairs])
    return jnp.concatenate([lower, cells, upper], axis=0)


def window_mask(block_lists, counts, head_ids, base, blocks):
    span = 2 * MARGIN + 1
    list_length = block_lists.shape[2]
    head_lists = jnp.take(block_lists, head_ids, axis=0)
    head_counts = jnp.take(counts, head_ids, axis=0)
    global_ids = base[:, None] + jnp.arange(blocks, dtype=jnp.int32)[None, :]
    lists = jnp.take_along_axis(head_lists, global_ids[:, :, None], axis=1)
    used = jnp.take_along_axis(head_counts, global_ids, axis=1)
    wanted = global_ids[:, :, None] + jnp.arange(span, dtype=jnp.int32)[None, None, :] - MARGIN
    live = jnp.arange(list_length, dtype=jnp.int32)[None, None, :] < used[:, :, None]
    hit = (lists[:, :, None, :] == wanted[:, :, :, None]) & live[:, :, None, :]
    return jnp.any(hit, axis=-1)


def attend(query_rows, key_ext, value_ext, allowed, logit_scale, value_factor):
    rows, heads, width = query_rows.shape
    blocks = rows // BLOCK
    span = 2 * MARGIN + 1
    q = query_rows.reshape(blocks, BLOCK, heads, width)
    kb = key_ext.reshape(blocks + 2 * MARGIN, BLOCK, heads, width)
    vb = value_ext.reshape(blocks + 2 * MARGIN, BLOCK, heads, width)
    kw = jnp.stack([kb[o : o + blocks] for o in range(span)], axis=1)
    vw = jnp.stack([vb[o : o + blocks] for o in range(span)], axis=1)
    logits = jnp.einsum("bqhd,bokhd->hbqok", q, kw, preferred_element_type=jnp.float32)
    logits = logits * logit_scale[:, None, None, None, None]
    logits = jnp.where(allowed[:, :, None, :, None], logits, -jnp.inf)
    peak = jnp.max(logits, axis=(3, 4), keepdims=True)
    weight = jnp.exp(logits - peak)
    total = jnp.sum(weight, axis=(3, 4))
    mixed = jnp.einsum(
        "hbqok,bokhd->bqhd", weight.astype(jnp.bfloat16), vw, preferred_element_type=jnp.float32
    )
    factor = value_factor[:, None, None] / total
    out = mixed * jnp.transpose(factor, (1, 2, 0))[:, :, :, None]
    return out.astype(jnp.bfloat16).reshape(rows, heads, width)


def shards(
    queries,
    key_vectors,
    value_vectors,
    labels,
    block_lists,
    counts,
    query_scale,
    key_scale,
    value_scale,
):
    groups = lax.axis_size("x")
    halves = lax.axis_size("zh")
    frames = lax.axis_size("frame")
    quarters = lax.axis_size("quarter")
    tokens_here = queries.shape[0]
    head_count = labels.shape[0]
    width = queries.shape[1] // head_count
    per_group = head_count // groups
    lines_per_group = TEMPORAL // groups
    spaces_per_group = per_group - lines_per_group
    rows = tokens_here * groups
    blocks = rows // BLOCK
    piece = rows // frames
    chunks = frames * quarters * halves

    group_index = lax.axis_index("x")
    half_index = lax.axis_index("zh")
    frame_index = lax.axis_index("frame")
    quarter_index = lax.axis_index("quarter")
    spatial_slot = (frame_index * quarters + quarter_index) * halves + half_index
    own_piece = (frame_index % 2) * (frames // 2) + frame_index // 2
    temporal_slot = (quarter_index * halves + half_index) * frames + own_piece

    heads = jnp.arange(head_count, dtype=jnp.int32)
    earlier = heads[None, :] < heads[:, None]
    is_line = labels == 1
    line_rank = jnp.sum(jnp.where(earlier, is_line[None, :], False), axis=1, dtype=jnp.int32)
    space_rank = heads - line_rank
    unslots = jnp.where(
        is_line,
        (line_rank // lines_per_group) * per_group + line_rank % lines_per_group,
        (space_rank // spaces_per_group) * per_group + lines_per_group + space_rank % spaces_per_group,
    )
    slots = jnp.sum(jnp.where(unslots[None, :] == heads[:, None], heads[None, :], 0), axis=1)

    columns = jnp.concatenate(
        [
            queries.reshape(tokens_here, head_count, width),
            key_vectors.reshape(tokens_here, head_count, width),
            value_vectors.reshape(tokens_here, head_count, width),
        ],
        axis=1,
    )
    grid = slots.reshape(groups, per_group)
    lo, hi = slice(0, lines_per_group), slice(lines_per_group, per_group)
    order = jnp.concatenate(
        [grid[:, lo] + t * head_count for t in range(3)] + [grid[:, hi] + t * head_count for t in range(3)],
        axis=1,
    )
    stacked = jnp.take(columns, order.reshape(-1), axis=1).reshape(
        tokens_here, groups, 3 * per_group, width
    )
    frame_rows = lax.all_to_all(stacked, "x", split_axis=1, concat_axis=0, tiled=True)
    frame_rows = frame_rows.reshape(rows, 3 * per_group, width)
    line_part = frame_rows[:, : 3 * lines_per_group]
    space_part = frame_rows[:, 3 * lines_per_group :]
    pairs = 2
    rings = frames // pairs
    pieces = line_part.reshape(pairs, rings, piece, 3 * lines_per_group, width)
    moved = lax.all_to_all(
        jnp.transpose(pieces, (1, 0, 2, 3, 4)).reshape(frames, piece, 3 * lines_per_group, width),
        "frame",
        split_axis=0,
        concat_axis=0,
        tiled=True,
    )
    space_kv = space_part[:, spaces_per_group:]
    moved, space_kv = lax.optimization_barrier((moved, space_kv))
    line_rows = jnp.transpose(moved, (1, 0, 2, 3)).reshape(rows, 3 * lines_per_group, width)

    def linear(half, frame, quarter):
        return (half * frames + frame) * quarters + quarter

    spatial_order = [
        linear(k % halves, k // (halves * quarters), (k // halves) % quarters) for k in range(chunks)
    ]
    temporal_order = [
        linear((k // frames) % halves, (k % rings) * pairs + (k % frames) // rings, k // (frames * halves))
        for k in range(chunks)
    ]
    along = ("zh", "frame", "quarter")
    space_ext = with_halo(space_kv, along, spatial_order)
    line_ext = with_halo(line_rows[:, lines_per_group:], along, temporal_order)

    group_heads = lax.dynamic_slice_in_dim(slots, group_index * per_group, per_group)
    logit_scale = (
        jnp.take(query_scale, group_heads) * jnp.take(key_scale, group_heads) / math.sqrt(width)
    )
    value_factor = jnp.take(value_scale, group_heads)

    def run(part_rows, ext, heads, base):
        n = heads.stop - heads.start
        ids = group_heads[heads]
        allowed = window_mask(
            block_lists, counts, ids, jnp.full((n,), base * blocks, jnp.int32), blocks
        )
        return attend(
            part_rows[:, :n], ext[:, :n], ext[:, n:], allowed, logit_scale[heads], value_factor[heads]
        )

    line_out = run(line_rows, line_ext, lo, temporal_slot)
    back = jnp.transpose(line_out.reshape(piece, frames, lines_per_group, width), (1, 0, 2, 3))
    back, space_ext = lax.optimization_barrier((back, space_ext))
    space_out = run(space_part, space_ext, hi, spatial_slot)

    returned = lax.all_to_all(back, "frame", split_axis=0, concat_axis=0, tiled=True)
    returned = jnp.transpose(
        returned.reshape(rings, pairs, piece, lines_per_group, width), (1, 0, 2, 3, 4)
    ).reshape(rows, lines_per_group, width)
    frame_outputs = jnp.concatenate([returned, space_out], axis=1)
    merged = lax.all_to_all(
        frame_outputs.reshape(rows, 1, per_group, width),
        "x",
        split_axis=0,
        concat_axis=1,
        tiled=True,
    )
    merged = jnp.take(merged.reshape(tokens_here, head_count, width), unslots, axis=1)
    return merged.reshape(tokens_here, head_count * width)


def solution(mesh):
    ulysses, context = mesh.devices.shape
    halves = mesh.devices.size // (context * HEAD_SPLIT)
    fine = Mesh(
        mesh.devices.reshape(halves, HEAD_SPLIT, FRAMES, context // FRAMES),
        ("zh", "x", "frame", "quarter"),
    )
    rows = P(("frame", "quarter", "zh", "x"), None)
    placed = (rows, rows, rows, P(), P(), P(), P(), P(), P())
    return jax.shard_map(
        shards,
        mesh=fine,
        in_specs=placed,
        out_specs=rows,
        check_vma=False,
    )
```

```python
import math

import jax
import jax.numpy as jnp
from jax import lax
from jax.sharding import Mesh, PartitionSpec as P

FRAMES = 16
MARGIN = 2
BLOCK = 64
TEMPORAL = 16
HEAD_SPLIT = 4


def with_halo(cells, axes, order):
    width = MARGIN * BLOCK
    pairs = list(zip(order[:-1], order[1:]))
    lower = lax.ppermute(cells[-width:], axes, pairs)
    upper = lax.ppermute(cells[:width], axes, [(b, a) for a, b in pairs])
    return jnp.concatenate([lower, cells, upper], axis=0)


def window_mask(block_lists, counts, head_ids, base, blocks):
    span = 2 * MARGIN + 1
    list_length = block_lists.shape[2]
    head_lists = jnp.take(block_lists, head_ids, axis=0)
    head_counts = jnp.take(counts, head_ids, axis=0)
    global_ids = base[:, None] + jnp.arange(blocks, dtype=jnp.int32)[None, :]
    lists = jnp.take_along_axis(head_lists, global_ids[:, :, None], axis=1)
    used = jnp.take_along_axis(head_counts, global_ids, axis=1)
    wanted = global_ids[:, :, None] + jnp.arange(span, dtype=jnp.int32)[None, None, :] - MARGIN
    live = jnp.arange(list_length, dtype=jnp.int32)[None, None, :] < used[:, :, None]
    hit = (lists[:, :, None, :] == wanted[:, :, :, None]) & live[:, :, None, :]
    return jnp.any(hit, axis=-1)


def attend(query_rows, key_ext, value_ext, allowed, logit_scale, value_factor):
    rows, heads, width = query_rows.shape
    blocks = rows // BLOCK
    span = 2 * MARGIN + 1
    q = query_rows.reshape(blocks, BLOCK, heads, width)
    kb = key_ext.reshape(blocks + 2 * MARGIN, BLOCK, heads, width)
    vb = value_ext.reshape(blocks + 2 * MARGIN, BLOCK, heads, width)
    kw = jnp.stack([kb[o : o + blocks] for o in range(span)], axis=1)
    vw = jnp.stack([vb[o : o + blocks] for o in range(span)], axis=1)
    logits = jnp.einsum("bqhd,bokhd->hbqok", q, kw, preferred_element_type=jnp.float32)
    logits = logits * logit_scale[:, None, None, None, None]
    logits = jnp.where(allowed[:, :, None, :, None], logits, -jnp.inf)
    peak = jnp.max(logits, axis=(3, 4), keepdims=True)
    weight = jnp.exp(logits - peak)
    total = jnp.sum(weight, axis=(3, 4))
    mixed = jnp.einsum(
        "hbqok,bokhd->bqhd", weight.astype(jnp.bfloat16), vw, preferred_element_type=jnp.float32
    )
    factor = value_factor[:, None, None] / total
    out = mixed * jnp.transpose(factor, (1, 2, 0))[:, :, :, None]
    return out.astype(jnp.bfloat16).reshape(rows, heads, width)


def shards(
    queries,
    key_vectors,
    value_vectors,
    labels,
    block_lists,
    counts,
    query_scale,
    key_scale,
    value_scale,
):
    groups = lax.axis_size("x")
    halves = lax.axis_size("zh")
    frames = lax.axis_size("frame")
    quarters = lax.axis_size("quarter")
    tokens_here = queries.shape[0]
    head_count = labels.shape[0]
    width = queries.shape[1] // head_count
    per_group = head_count // groups
    lines_per_group = TEMPORAL // groups
    spaces_per_group = per_group - lines_per_group
    rows = tokens_here * groups
    blocks = rows // BLOCK
    piece = rows // frames
    chunks = frames * quarters * halves

    group_index = lax.axis_index("x")
    half_index = lax.axis_index("zh")
    frame_index = lax.axis_index("frame")
    quarter_index = lax.axis_index("quarter")
    spatial_slot = (frame_index * quarters + quarter_index) * halves + half_index
    own_piece = (frame_index % 2) * (frames // 2) + frame_index // 2
    temporal_slot = (quarter_index * halves + half_index) * frames + own_piece

    heads = jnp.arange(head_count, dtype=jnp.int32)
    earlier = heads[None, :] < heads[:, None]
    is_line = labels == 1
    line_rank = jnp.sum(jnp.where(earlier, is_line[None, :], False), axis=1, dtype=jnp.int32)
    space_rank = heads - line_rank
    unslots = jnp.where(
        is_line,
        (line_rank // lines_per_group) * per_group + line_rank % lines_per_group,
        (space_rank // spaces_per_group) * per_group + lines_per_group + space_rank % spaces_per_group,
    )
    slots = jnp.sum(jnp.where(unslots[None, :] == heads[:, None], heads[None, :], 0), axis=1)

    columns = jnp.concatenate(
        [
            queries.reshape(tokens_here, head_count, width),
            key_vectors.reshape(tokens_here, head_count, width),
            value_vectors.reshape(tokens_here, head_count, width),
        ],
        axis=1,
    )
    grid = slots.reshape(groups, per_group)
    lo, hi = slice(0, lines_per_group), slice(lines_per_group, per_group)
    order = jnp.concatenate(
        [grid[:, lo] + t * head_count for t in range(3)] + [grid[:, hi] + t * head_count for t in range(3)],
        axis=1,
    )
    picks = (
        order.reshape(-1)[:, None] == jnp.arange(3 * head_count, dtype=jnp.int32)[None, :]
    ).astype(jnp.bfloat16)
    stacked = jnp.einsum(
        "sh,thd->tsd", picks, columns, preferred_element_type=jnp.bfloat16
    ).reshape(tokens_here, groups, 3 * per_group, width)
    frame_rows = lax.all_to_all(stacked, "x", split_axis=1, concat_axis=0, tiled=True)
    frame_rows = frame_rows.reshape(rows, 3 * per_group, width)
    line_part = frame_rows[:, : 3 * lines_per_group]
    space_part = frame_rows[:, 3 * lines_per_group :]
    pairs = 2
    rings = frames // pairs
    pieces = line_part.reshape(pairs, rings, piece, 3 * lines_per_group, width)
    moved = lax.all_to_all(
        jnp.transpose(pieces, (1, 0, 2, 3, 4)).reshape(frames, piece, 3 * lines_per_group, width),
        "frame",
        split_axis=0,
        concat_axis=0,
        tiled=True,
    )
    space_kv = space_part[:, spaces_per_group:]
    moved, space_kv = lax.optimization_barrier((moved, space_kv))
    line_rows = jnp.transpose(moved, (1, 0, 2, 3)).reshape(rows, 3 * lines_per_group, width)

    def linear(half, frame, quarter):
        return (half * frames + frame) * quarters + quarter

    spatial_order = [
        linear(k % halves, k // (halves * quarters), (k // halves) % quarters) for k in range(chunks)
    ]
    temporal_order = [
        linear((k // frames) % halves, (k % rings) * pairs + (k % frames) // rings, k // (frames * halves))
        for k in range(chunks)
    ]
    along = ("zh", "frame", "quarter")
    space_ext = with_halo(space_kv, along, spatial_order)
    line_ext = with_halo(line_rows[:, lines_per_group:], along, temporal_order)

    group_heads = lax.dynamic_slice_in_dim(slots, group_index * per_group, per_group)
    logit_scale = (
        jnp.take(query_scale, group_heads) * jnp.take(key_scale, group_heads) / math.sqrt(width)
    )
    value_factor = jnp.take(value_scale, group_heads)

    def run(part_rows, ext, heads, base):
        n = heads.stop - heads.start
        ids = group_heads[heads]
        allowed = window_mask(
            block_lists, counts, ids, jnp.full((n,), base * blocks, jnp.int32), blocks
        )
        return attend(
            part_rows[:, :n], ext[:, :n], ext[:, n:], allowed, logit_scale[heads], value_factor[heads]
        )

    line_out = run(line_rows, line_ext, lo, temporal_slot)
    back = jnp.transpose(line_out.reshape(piece, frames, lines_per_group, width), (1, 0, 2, 3))
    back, space_ext = lax.optimization_barrier((back, space_ext))
    space_out = run(space_part, space_ext, hi, spatial_slot)

    returned = lax.all_to_all(back, "frame", split_axis=0, concat_axis=0, tiled=True)
    returned = jnp.transpose(
        returned.reshape(rings, pairs, piece, lines_per_group, width), (1, 0, 2, 3, 4)
    ).reshape(rows, lines_per_group, width)
    frame_outputs = jnp.concatenate([returned, space_out], axis=1)
    merged = lax.all_to_all(
        frame_outputs.reshape(rows, 1, per_group, width),
        "x",
        split_axis=0,
        concat_axis=1,
        tiled=True,
    )
    merged = jnp.take(merged.reshape(tokens_here, head_count, width), unslots, axis=1)
    return merged.reshape(tokens_here, head_count * width)


def solution(mesh):
    ulysses, context = mesh.devices.shape
    halves = mesh.devices.size // (context * HEAD_SPLIT)
    fine = Mesh(
        mesh.devices.reshape(halves, HEAD_SPLIT, FRAMES, context // FRAMES),
        ("zh", "x", "frame", "quarter"),
    )
    rows = P(("frame", "quarter", "zh", "x"), None)
    placed = (rows, rows, rows, P(), P(), P(), P(), P(), P())
    return jax.shard_map(
        shards,
        mesh=fine,
        in_specs=placed,
        out_specs=rows,
        check_vma=False,
    )
```

```python
import math

import jax
import jax.numpy as jnp
from jax import lax
from jax.sharding import Mesh, PartitionSpec as P

FRAMES = 16
MARGIN = 2
BLOCK = 64
TEMPORAL = 16
HEAD_SPLIT = 4


def with_halo(cells, axes, order):
    width = MARGIN * BLOCK
    pairs = list(zip(order[:-1], order[1:]))
    lower = lax.ppermute(cells[-width:], axes, pairs)
    upper = lax.ppermute(cells[:width], axes, [(b, a) for a, b in pairs])
    return jnp.concatenate([lower, cells, upper], axis=0)


def window_mask(block_lists, counts, head_ids, base, blocks):
    span = 2 * MARGIN + 1
    list_length = block_lists.shape[2]
    head_lists = jnp.take(block_lists, head_ids, axis=0)
    head_counts = jnp.take(counts, head_ids, axis=0)
    global_ids = base[:, None] + jnp.arange(blocks, dtype=jnp.int32)[None, :]
    lists = jnp.take_along_axis(head_lists, global_ids[:, :, None], axis=1)
    used = jnp.take_along_axis(head_counts, global_ids, axis=1)
    wanted = global_ids[:, :, None] + jnp.arange(span, dtype=jnp.int32)[None, None, :] - MARGIN
    live = jnp.arange(list_length, dtype=jnp.int32)[None, None, :] < used[:, :, None]
    hit = (lists[:, :, None, :] == wanted[:, :, :, None]) & live[:, :, None, :]
    return jnp.any(hit, axis=-1)


def attend(query_rows, key_ext, value_ext, allowed, logit_scale, value_factor):
    rows, heads, width = query_rows.shape
    blocks = rows // BLOCK
    span = 2 * MARGIN + 1
    q = query_rows.reshape(blocks, BLOCK, heads, width)
    kb = key_ext.reshape(blocks + 2 * MARGIN, BLOCK, heads, width)
    vb = value_ext.reshape(blocks + 2 * MARGIN, BLOCK, heads, width)
    kw = jnp.stack([kb[o : o + blocks] for o in range(span)], axis=1)
    vw = jnp.stack([vb[o : o + blocks] for o in range(span)], axis=1)
    logits = jnp.einsum("bqhd,bokhd->hbqok", q, kw, preferred_element_type=jnp.float32)
    logits = logits * logit_scale[:, None, None, None, None]
    logits = jnp.where(allowed[:, :, None, :, None], logits, -jnp.inf)
    peak = jnp.max(logits, axis=(3, 4), keepdims=True)
    weight = jnp.exp(logits - peak)
    total = jnp.sum(weight, axis=(3, 4))
    mixed = jnp.einsum(
        "hbqok,bokhd->bqhd", weight.astype(jnp.bfloat16), vw, preferred_element_type=jnp.float32
    )
    factor = value_factor[:, None, None] / total
    out = mixed * jnp.transpose(factor, (1, 2, 0))[:, :, :, None]
    return out.astype(jnp.bfloat16).reshape(rows, heads, width)


def shards(
    queries,
    key_vectors,
    value_vectors,
    labels,
    block_lists,
    counts,
    query_scale,
    key_scale,
    value_scale,
):
    groups = lax.axis_size("x")
    halves = lax.axis_size("zh")
    frames = lax.axis_size("frame")
    quarters = lax.axis_size("quarter")
    tokens_here = queries.shape[0]
    head_count = labels.shape[0]
    width = queries.shape[1] // head_count
    per_group = head_count // groups
    lines_per_group = TEMPORAL // groups
    spaces_per_group = per_group - lines_per_group
    rows = tokens_here * groups
    blocks = rows // BLOCK
    piece = rows // frames
    chunks = frames * quarters * halves

    group_index = lax.axis_index("x")
    half_index = lax.axis_index("zh")
    frame_index = lax.axis_index("frame")
    quarter_index = lax.axis_index("quarter")
    spatial_slot = (frame_index * quarters + quarter_index) * halves + half_index
    own_piece = (frame_index % 2) * (frames // 2) + frame_index // 2
    temporal_slot = (quarter_index * halves + half_index) * frames + own_piece

    heads = jnp.arange(head_count, dtype=jnp.int32)
    earlier = heads[None, :] < heads[:, None]
    is_line = labels == 1
    line_rank = jnp.sum(jnp.where(earlier, is_line[None, :], False), axis=1, dtype=jnp.int32)
    space_rank = heads - line_rank
    unslots = jnp.where(
        is_line,
        (line_rank // lines_per_group) * per_group + line_rank % lines_per_group,
        (space_rank // spaces_per_group) * per_group + lines_per_group + space_rank % spaces_per_group,
    )
    slots = jnp.sum(jnp.where(unslots[None, :] == heads[:, None], heads[None, :], 0), axis=1)

    columns = jnp.concatenate(
        [
            queries.reshape(tokens_here, head_count, width),
            key_vectors.reshape(tokens_here, head_count, width),
            value_vectors.reshape(tokens_here, head_count, width),
        ],
        axis=1,
    )
    grid = slots.reshape(groups, per_group)
    lo, hi = slice(0, lines_per_group), slice(lines_per_group, per_group)
    order = jnp.concatenate(
        [grid[:, lo] + t * head_count for t in range(3)] + [grid[:, hi] + t * head_count for t in range(3)],
        axis=1,
    )
    picks = (
        order.reshape(-1)[:, None] == jnp.arange(3 * head_count, dtype=jnp.int32)[None, :]
    ).astype(jnp.bfloat16)
    stacked = jnp.einsum(
        "sh,thd->tsd", picks, columns, preferred_element_type=jnp.bfloat16
    ).reshape(tokens_here, groups, 3 * per_group, width)
    frame_rows = lax.all_to_all(stacked, "x", split_axis=1, concat_axis=0, tiled=True)
    frame_rows = frame_rows.reshape(rows, 3 * per_group, width)
    line_part = frame_rows[:, : 3 * lines_per_group]
    space_part = frame_rows[:, 3 * lines_per_group :]
    pairs = 2
    rings = frames // pairs
    pieces = line_part.reshape(pairs, rings, piece, 3 * lines_per_group, width)
    moved = lax.all_to_all(
        jnp.transpose(pieces, (1, 0, 2, 3, 4)).reshape(frames, piece, 3 * lines_per_group, width),
        "frame",
        split_axis=0,
        concat_axis=0,
        tiled=True,
    )
    space_kv = space_part[:, spaces_per_group:]
    moved, space_kv = lax.optimization_barrier((moved, space_kv))
    line_rows = jnp.transpose(moved, (1, 0, 2, 3)).reshape(rows, 3 * lines_per_group, width)

    def linear(half, frame, quarter):
        return (half * frames + frame) * quarters + quarter

    spatial_order = [
        linear(k % halves, k // (halves * quarters), (k // halves) % quarters) for k in range(chunks)
    ]
    temporal_order = [
        linear((k // frames) % halves, (k % rings) * pairs + (k % frames) // rings, k // (frames * halves))
        for k in range(chunks)
    ]
    along = ("zh", "frame", "quarter")
    space_ext = with_halo(space_kv, along, spatial_order)
    line_ext = with_halo(line_rows[:, lines_per_group:], along, temporal_order)

    group_heads = lax.dynamic_slice_in_dim(slots, group_index * per_group, per_group)
    logit_scale = (
        jnp.take(query_scale, group_heads) * jnp.take(key_scale, group_heads) / math.sqrt(width)
    )
    value_factor = jnp.take(value_scale, group_heads)

    def run(part_rows, ext, heads, base):
        n = heads.stop - heads.start
        ids = group_heads[heads]
        allowed = window_mask(
            block_lists, counts, ids, jnp.full((n,), base * blocks, jnp.int32), blocks
        )
        return attend(
            part_rows[:, :n], ext[:, :n], ext[:, n:], allowed, logit_scale[heads], value_factor[heads]
        )

    line_out = run(line_rows, line_ext, lo, temporal_slot)
    back = jnp.transpose(line_out.reshape(piece, frames, lines_per_group, width), (1, 0, 2, 3))
    space_out = run(space_part, space_ext, hi, spatial_slot)

    returned = lax.all_to_all(back, "frame", split_axis=0, concat_axis=0, tiled=True)
    returned = jnp.transpose(
        returned.reshape(rings, pairs, piece, lines_per_group, width), (1, 0, 2, 3, 4)
    ).reshape(rows, lines_per_group, width)
    frame_outputs = jnp.concatenate([returned, space_out], axis=1)
    merged = lax.all_to_all(
        frame_outputs.reshape(rows, 1, per_group, width),
        "x",
        split_axis=0,
        concat_axis=1,
        tiled=True,
    )
    merged = jnp.take(merged.reshape(tokens_here, head_count, width), unslots, axis=1)
    return merged.reshape(tokens_here, head_count * width)


def solution(mesh):
    ulysses, context = mesh.devices.shape
    halves = mesh.devices.size // (context * HEAD_SPLIT)
    fine = Mesh(
        mesh.devices.reshape(halves, HEAD_SPLIT, FRAMES, context // FRAMES),
        ("zh", "x", "frame", "quarter"),
    )
    rows = P(("frame", "quarter", "zh", "x"), None)
    placed = (rows, rows, rows, P(), P(), P(), P(), P(), P())
    return jax.shard_map(
        shards,
        mesh=fine,
        in_specs=placed,
        out_specs=rows,
        check_vma=False,
    )
```

```python
import math

import jax
import jax.numpy as jnp
from jax import lax
from jax.sharding import Mesh, PartitionSpec as P

FRAMES = 16
MARGIN = 2
BLOCK = 64
TEMPORAL = 16
HEAD_SPLIT = 4


def with_halo(cells, axes, order):
    width = MARGIN * BLOCK
    pairs = list(zip(order[:-1], order[1:]))
    lower = lax.ppermute(cells[-width:], axes, pairs)
    upper = lax.ppermute(cells[:width], axes, [(b, a) for a, b in pairs])
    return jnp.concatenate([lower, cells, upper], axis=0)


def window_mask(block_lists, counts, head_ids, base, blocks):
    span = 2 * MARGIN + 1
    list_length = block_lists.shape[2]
    head_lists = jnp.take(block_lists, head_ids, axis=0)
    head_counts = jnp.take(counts, head_ids, axis=0)
    global_ids = base[:, None] + jnp.arange(blocks, dtype=jnp.int32)[None, :]
    lists = jnp.take_along_axis(head_lists, global_ids[:, :, None], axis=1)
    used = jnp.take_along_axis(head_counts, global_ids, axis=1)
    wanted = global_ids[:, :, None] + jnp.arange(span, dtype=jnp.int32)[None, None, :] - MARGIN
    live = jnp.arange(list_length, dtype=jnp.int32)[None, None, :] < used[:, :, None]
    hit = (lists[:, :, None, :] == wanted[:, :, :, None]) & live[:, :, None, :]
    return jnp.any(hit, axis=-1)


def attend(query_rows, key_ext, value_ext, allowed, logit_scale, value_factor):
    rows, heads, width = query_rows.shape
    blocks = rows // BLOCK
    span = 2 * MARGIN + 1
    q = query_rows.reshape(blocks, BLOCK, heads, width)
    kb = key_ext.reshape(blocks + 2 * MARGIN, BLOCK, heads, width)
    vb = value_ext.reshape(blocks + 2 * MARGIN, BLOCK, heads, width)
    kw = jnp.stack([kb[o : o + blocks] for o in range(span)], axis=1)
    vw = jnp.stack([vb[o : o + blocks] for o in range(span)], axis=1)
    logits = jnp.einsum("bqhd,bokhd->hbqok", q, kw, preferred_element_type=jnp.float32)
    logits = logits * logit_scale[:, None, None, None, None]
    logits = jnp.where(allowed[:, :, None, :, None], logits, -jnp.inf)
    peak = jnp.max(logits, axis=(3, 4), keepdims=True)
    weight = jnp.exp(logits - peak)
    total = jnp.sum(weight, axis=(3, 4))
    mixed = jnp.einsum(
        "hbqok,bokhd->bqhd", weight.astype(jnp.bfloat16), vw, preferred_element_type=jnp.float32
    )
    factor = value_factor[:, None, None] / total
    out = mixed * jnp.transpose(factor, (1, 2, 0))[:, :, :, None]
    return out.astype(jnp.bfloat16).reshape(rows, heads, width)


def shards(
    queries,
    key_vectors,
    value_vectors,
    labels,
    block_lists,
    counts,
    query_scale,
    key_scale,
    value_scale,
):
    groups = lax.axis_size("x")
    halves = lax.axis_size("zh")
    frames = lax.axis_size("frame")
    quarters = lax.axis_size("quarter")
    tokens_here = queries.shape[0]
    head_count = labels.shape[0]
    width = queries.shape[1] // head_count
    per_group = head_count // groups
    lines_per_group = TEMPORAL // groups
    spaces_per_group = per_group - lines_per_group
    rows = tokens_here * groups
    blocks = rows // BLOCK
    piece = rows // frames
    chunks = frames * quarters * halves

    group_index = lax.axis_index("x")
    half_index = lax.axis_index("zh")
    frame_index = lax.axis_index("frame")
    quarter_index = lax.axis_index("quarter")
    spatial_slot = (frame_index * quarters + quarter_index) * halves + half_index
    own_piece = (frame_index % 2) * (frames // 2) + frame_index // 2
    temporal_slot = (quarter_index * halves + half_index) * frames + own_piece

    heads = jnp.arange(head_count, dtype=jnp.int32)
    earlier = heads[None, :] < heads[:, None]
    is_line = labels == 1
    line_rank = jnp.sum(jnp.where(earlier, is_line[None, :], False), axis=1, dtype=jnp.int32)
    space_rank = heads - line_rank
    unslots = jnp.where(
        is_line,
        (line_rank // lines_per_group) * per_group + line_rank % lines_per_group,
        (space_rank // spaces_per_group) * per_group + lines_per_group + space_rank % spaces_per_group,
    )
    slots = jnp.sum(jnp.where(unslots[None, :] == heads[:, None], heads[None, :], 0), axis=1)

    columns = jnp.concatenate(
        [
            queries.reshape(tokens_here, head_count, width),
            key_vectors.reshape(tokens_here, head_count, width),
            value_vectors.reshape(tokens_here, head_count, width),
        ],
        axis=1,
    )
    grid = slots.reshape(groups, per_group)
    lo, hi = slice(0, lines_per_group), slice(lines_per_group, per_group)
    order = jnp.concatenate(
        [grid[:, lo] + t * head_count for t in range(3)] + [grid[:, hi] + t * head_count for t in range(3)],
        axis=1,
    )
    picks = (
        order.reshape(-1)[:, None] == jnp.arange(3 * head_count, dtype=jnp.int32)[None, :]
    ).astype(jnp.bfloat16)
    stacked = jnp.einsum(
        "sh,thd->tsd", picks, columns, preferred_element_type=jnp.bfloat16
    ).reshape(tokens_here, groups, 3 * per_group, width)
    frame_rows = lax.all_to_all(stacked, "x", split_axis=1, concat_axis=0, tiled=True)
    frame_rows = frame_rows.reshape(rows, 3 * per_group, width)
    line_part = frame_rows[:, : 3 * lines_per_group]
    space_part = frame_rows[:, 3 * lines_per_group :]
    pairs = 2
    rings = frames // pairs
    pieces = line_part.reshape(pairs, rings, piece, 3 * lines_per_group, width)
    moved = lax.all_to_all(
        jnp.transpose(pieces, (1, 0, 2, 3, 4)).reshape(frames, piece, 3 * lines_per_group, width),
        "frame",
        split_axis=0,
        concat_axis=0,
        tiled=True,
    )
    space_kv = space_part[:, spaces_per_group:]
    moved, space_kv = lax.optimization_barrier((moved, space_kv))
    line_rows = jnp.transpose(moved, (1, 0, 2, 3)).reshape(rows, 3 * lines_per_group, width)

    def linear(half, frame, quarter):
        return (half * frames + frame) * quarters + quarter

    spatial_order = [
        linear(k % halves, k // (halves * quarters), (k // halves) % quarters) for k in range(chunks)
    ]
    temporal_order = [
        linear((k // frames) % halves, (k % rings) * pairs + (k % frames) // rings, k // (frames * halves))
        for k in range(chunks)
    ]
    along = ("zh", "frame", "quarter")
    line_ext = with_halo(line_rows[:, lines_per_group:], along, temporal_order)
    line_ext, space_kv = lax.optimization_barrier((line_ext, space_kv))
    space_ext = with_halo(space_kv, along, spatial_order)

    group_heads = lax.dynamic_slice_in_dim(slots, group_index * per_group, per_group)
    logit_scale = (
        jnp.take(query_scale, group_heads) * jnp.take(key_scale, group_heads) / math.sqrt(width)
    )
    value_factor = jnp.take(value_scale, group_heads)

    def run(part_rows, ext, heads, base):
        n = heads.stop - heads.start
        ids = group_heads[heads]
        allowed = window_mask(
            block_lists, counts, ids, jnp.full((n,), base * blocks, jnp.int32), blocks
        )
        return attend(
            part_rows[:, :n], ext[:, :n], ext[:, n:], allowed, logit_scale[heads], value_factor[heads]
        )

    line_out = run(line_rows, line_ext, lo, temporal_slot)
    back = jnp.transpose(line_out.reshape(piece, frames, lines_per_group, width), (1, 0, 2, 3))
    space_out = run(space_part, space_ext, hi, spatial_slot)

    returned = lax.all_to_all(back, "frame", split_axis=0, concat_axis=0, tiled=True)
    returned = jnp.transpose(
        returned.reshape(rings, pairs, piece, lines_per_group, width), (1, 0, 2, 3, 4)
    ).reshape(rows, lines_per_group, width)
    frame_outputs = jnp.concatenate([returned, space_out], axis=1)
    merged = lax.all_to_all(
        frame_outputs.reshape(rows, 1, per_group, width),
        "x",
        split_axis=0,
        concat_axis=1,
        tiled=True,
    )
    merged = jnp.take(merged.reshape(tokens_here, head_count, width), unslots, axis=1)
    return merged.reshape(tokens_here, head_count * width)


def solution(mesh):
    ulysses, context = mesh.devices.shape
    halves = mesh.devices.size // (context * HEAD_SPLIT)
    fine = Mesh(
        mesh.devices.reshape(halves, HEAD_SPLIT, FRAMES, context // FRAMES),
        ("zh", "x", "frame", "quarter"),
    )
    rows = P(("frame", "quarter", "zh", "x"), None)
    placed = (rows, rows, rows, P(), P(), P(), P(), P(), P())
    return jax.shard_map(
        shards,
        mesh=fine,
        in_specs=placed,
        out_specs=rows,
        check_vma=False,
    )
```

```python
import math

import jax
import jax.numpy as jnp
from jax import lax
from jax.sharding import Mesh, PartitionSpec as P

FRAMES = 16
MARGIN = 2
BLOCK = 64
TEMPORAL = 16
HEAD_SPLIT = 4


def with_halo(cells, axes, order):
    width = MARGIN * BLOCK
    pairs = list(zip(order[:-1], order[1:]))
    lower = lax.ppermute(cells[-width:], axes, pairs)
    upper = lax.ppermute(cells[:width], axes, [(b, a) for a, b in pairs])
    return jnp.concatenate([lower, cells, upper], axis=0)


def window_mask(block_lists, counts, head_ids, base, blocks):
    span = 2 * MARGIN + 1
    list_length = block_lists.shape[2]
    head_lists = jnp.take(block_lists, head_ids, axis=0)
    head_counts = jnp.take(counts, head_ids, axis=0)
    global_ids = base[:, None] + jnp.arange(blocks, dtype=jnp.int32)[None, :]
    lists = jnp.take_along_axis(head_lists, global_ids[:, :, None], axis=1)
    used = jnp.take_along_axis(head_counts, global_ids, axis=1)
    wanted = global_ids[:, :, None] + jnp.arange(span, dtype=jnp.int32)[None, None, :] - MARGIN
    live = jnp.arange(list_length, dtype=jnp.int32)[None, None, :] < used[:, :, None]
    hit = (lists[:, :, None, :] == wanted[:, :, :, None]) & live[:, :, None, :]
    return jnp.any(hit, axis=-1)


def attend(query_rows, key_ext, value_ext, allowed, logit_scale, value_factor):
    rows, heads, width = query_rows.shape
    blocks = rows // BLOCK
    span = 2 * MARGIN + 1
    q = query_rows.reshape(blocks, BLOCK, heads, width)
    kb = key_ext.reshape(blocks + 2 * MARGIN, BLOCK, heads, width)
    vb = value_ext.reshape(blocks + 2 * MARGIN, BLOCK, heads, width)
    kw = jnp.stack([kb[o : o + blocks] for o in range(span)], axis=1)
    vw = jnp.stack([vb[o : o + blocks] for o in range(span)], axis=1)
    logits = jnp.einsum("bqhd,bokhd->hbqok", q, kw, preferred_element_type=jnp.float32)
    logits = logits * logit_scale[:, None, None, None, None]
    logits = jnp.where(allowed[:, :, None, :, None], logits, -jnp.inf)
    peak = jnp.max(logits, axis=(3, 4), keepdims=True)
    weight = jnp.exp(logits - peak)
    total = jnp.sum(weight, axis=(3, 4))
    mixed = jnp.einsum(
        "hbqok,bokhd->bqhd", weight.astype(jnp.bfloat16), vw, preferred_element_type=jnp.float32
    )
    factor = value_factor[:, None, None] / total
    out = mixed * jnp.transpose(factor, (1, 2, 0))[:, :, :, None]
    return out.astype(jnp.bfloat16).reshape(rows, heads, width)


def shards(
    queries,
    key_vectors,
    value_vectors,
    labels,
    block_lists,
    counts,
    query_scale,
    key_scale,
    value_scale,
):
    groups = lax.axis_size("x")
    halves = lax.axis_size("zh")
    frames = lax.axis_size("frame")
    quarters = lax.axis_size("quarter")
    tokens_here = queries.shape[0]
    head_count = labels.shape[0]
    width = queries.shape[1] // head_count
    per_group = head_count // groups
    lines_per_group = TEMPORAL // groups
    spaces_per_group = per_group - lines_per_group
    rows = tokens_here * groups
    blocks = rows // BLOCK
    piece = rows // frames
    chunks = frames * quarters * halves

    group_index = lax.axis_index("x")
    half_index = lax.axis_index("zh")
    frame_index = lax.axis_index("frame")
    quarter_index = lax.axis_index("quarter")
    spatial_slot = (frame_index * quarters + quarter_index) * halves + half_index
    own_piece = (frame_index % 2) * (frames // 2) + frame_index // 2
    temporal_slot = (quarter_index * halves + half_index) * frames + own_piece

    heads = jnp.arange(head_count, dtype=jnp.int32)
    earlier = heads[None, :] < heads[:, None]
    is_line = labels == 1
    line_rank = jnp.sum(jnp.where(earlier, is_line[None, :], False), axis=1, dtype=jnp.int32)
    space_rank = heads - line_rank
    unslots = jnp.where(
        is_line,
        (line_rank // lines_per_group) * per_group + line_rank % lines_per_group,
        (space_rank // spaces_per_group) * per_group + lines_per_group + space_rank % spaces_per_group,
    )
    slots = jnp.sum(jnp.where(unslots[None, :] == heads[:, None], heads[None, :], 0), axis=1)

    columns = jnp.concatenate(
        [
            queries.reshape(tokens_here, head_count, width),
            key_vectors.reshape(tokens_here, head_count, width),
            value_vectors.reshape(tokens_here, head_count, width),
        ],
        axis=1,
    )
    grid = slots.reshape(groups, per_group)
    lo, hi = slice(0, lines_per_group), slice(lines_per_group, per_group)
    order = jnp.concatenate(
        [grid[:, lo] + t * head_count for t in range(3)] + [grid[:, hi] + t * head_count for t in range(3)],
        axis=1,
    )
    picks = (
        order[:, :, None] == jnp.arange(3 * head_count, dtype=jnp.int32)[None, None, :]
    ).astype(jnp.bfloat16)
    stacked = jnp.einsum("gsh,thd->gtsd", picks, columns, preferred_element_type=jnp.bfloat16)
    frame_rows = lax.all_to_all(stacked, "x", split_axis=0, concat_axis=0, tiled=True)
    frame_rows = frame_rows.reshape(rows, 3 * per_group, width)
    line_part = frame_rows[:, : 3 * lines_per_group]
    space_part = frame_rows[:, 3 * lines_per_group :]
    pairs = 2
    rings = frames // pairs
    pieces = line_part.reshape(pairs, rings, piece, 3 * lines_per_group, width)
    moved = lax.all_to_all(
        jnp.transpose(pieces, (1, 0, 2, 3, 4)).reshape(frames, piece, 3 * lines_per_group, width),
        "frame",
        split_axis=0,
        concat_axis=0,
        tiled=True,
    )
    space_kv = space_part[:, spaces_per_group:]
    moved, space_kv = lax.optimization_barrier((moved, space_kv))
    line_rows = jnp.transpose(moved, (1, 0, 2, 3)).reshape(rows, 3 * lines_per_group, width)

    def linear(half, frame, quarter):
        return (half * frames + frame) * quarters + quarter

    spatial_order = [
        linear(k % halves, k // (halves * quarters), (k // halves) % quarters) for k in range(chunks)
    ]
    temporal_order = [
        linear((k // frames) % halves, (k % rings) * pairs + (k % frames) // rings, k // (frames * halves))
        for k in range(chunks)
    ]
    along = ("zh", "frame", "quarter")
    space_ext = with_halo(space_kv, along, spatial_order)
    line_ext = with_halo(line_rows[:, lines_per_group:], along, temporal_order)

    group_heads = lax.dynamic_slice_in_dim(slots, group_index * per_group, per_group)
    logit_scale = (
        jnp.take(query_scale, group_heads) * jnp.take(key_scale, group_heads) / math.sqrt(width)
    )
    value_factor = jnp.take(value_scale, group_heads)

    def run(part_rows, ext, heads, base):
        n = heads.stop - heads.start
        ids = group_heads[heads]
        allowed = window_mask(
            block_lists, counts, ids, jnp.full((n,), base * blocks, jnp.int32), blocks
        )
        return attend(
            part_rows[:, :n], ext[:, :n], ext[:, n:], allowed, logit_scale[heads], value_factor[heads]
        )

    line_out = run(line_rows, line_ext, lo, temporal_slot)
    back = jnp.transpose(line_out.reshape(piece, frames, lines_per_group, width), (1, 0, 2, 3))
    space_out = run(space_part, space_ext, hi, spatial_slot)

    returned = lax.all_to_all(back, "frame", split_axis=0, concat_axis=0, tiled=True)
    returned = jnp.transpose(
        returned.reshape(rings, pairs, piece, lines_per_group, width), (1, 0, 2, 3, 4)
    ).reshape(rows, lines_per_group, width)
    frame_outputs = jnp.concatenate([returned, space_out], axis=1)
    merged = lax.all_to_all(
        frame_outputs.reshape(groups, tokens_here, per_group, width),
        "x",
        split_axis=0,
        concat_axis=0,
        tiled=True,
    )
    places = (
        unslots[:, None] == jnp.arange(head_count, dtype=jnp.int32)[None, :]
    ).astype(jnp.bfloat16).reshape(head_count, groups, per_group)
    merged = jnp.einsum("hgs,gtsd->thd", places, merged, preferred_element_type=jnp.bfloat16)
    return merged.reshape(tokens_here, head_count * width)


def solution(mesh):
    ulysses, context = mesh.devices.shape
    halves = mesh.devices.size // (context * HEAD_SPLIT)
    fine = Mesh(
        mesh.devices.reshape(halves, HEAD_SPLIT, FRAMES, context // FRAMES),
        ("zh", "x", "frame", "quarter"),
    )
    rows = P(("frame", "quarter", "zh", "x"), None)
    placed = (rows, rows, rows, P(), P(), P(), P(), P(), P())
    return jax.shard_map(
        shards,
        mesh=fine,
        in_specs=placed,
        out_specs=rows,
        check_vma=False,
    )
```

```python
import math

import jax
import jax.numpy as jnp
from jax import lax
from jax.sharding import Mesh, PartitionSpec as P

FRAMES = 16
MARGIN = 2
BLOCK = 64
TEMPORAL = 16
HEAD_SPLIT = 4


def with_halo(cells, axes, order):
    width = MARGIN * BLOCK
    pairs = list(zip(order[:-1], order[1:]))
    lower = lax.ppermute(cells[-width:], axes, pairs)
    upper = lax.ppermute(cells[:width], axes, [(b, a) for a, b in pairs])
    return jnp.concatenate([lower, cells, upper], axis=0)


def window_mask(block_lists, counts, head_ids, base, blocks):
    span = 2 * MARGIN + 1
    list_length = block_lists.shape[2]
    head_lists = jnp.take(block_lists, head_ids, axis=0)
    head_counts = jnp.take(counts, head_ids, axis=0)
    global_ids = base[:, None] + jnp.arange(blocks, dtype=jnp.int32)[None, :]
    lists = jnp.take_along_axis(head_lists, global_ids[:, :, None], axis=1)
    used = jnp.take_along_axis(head_counts, global_ids, axis=1)
    wanted = global_ids[:, :, None] + jnp.arange(span, dtype=jnp.int32)[None, None, :] - MARGIN
    live = jnp.arange(list_length, dtype=jnp.int32)[None, None, :] < used[:, :, None]
    hit = (lists[:, :, None, :] == wanted[:, :, :, None]) & live[:, :, None, :]
    return jnp.any(hit, axis=-1)


def attend(query_rows, key_ext, value_ext, allowed, logit_scale, value_factor):
    rows, heads, width = query_rows.shape
    blocks = rows // BLOCK
    span = 2 * MARGIN + 1
    q = query_rows.reshape(blocks, BLOCK, heads, width)
    kb = key_ext.reshape(blocks + 2 * MARGIN, BLOCK, heads, width)
    vb = value_ext.reshape(blocks + 2 * MARGIN, BLOCK, heads, width)
    kw = jnp.stack([kb[o : o + blocks] for o in range(span)], axis=1)
    vw = jnp.stack([vb[o : o + blocks] for o in range(span)], axis=1)
    logits = jnp.einsum("bqhd,bokhd->hbqok", q, kw, preferred_element_type=jnp.float32)
    logits = logits * logit_scale[:, None, None, None, None]
    logits = jnp.where(allowed[:, :, None, :, None], logits, -jnp.inf)
    peak = jnp.max(logits, axis=(3, 4), keepdims=True)
    weight = jnp.exp(logits - peak)
    total = jnp.sum(weight, axis=(3, 4))
    mixed = jnp.einsum(
        "hbqok,bokhd->bqhd", weight.astype(jnp.bfloat16), vw, preferred_element_type=jnp.float32
    )
    factor = value_factor[:, None, None] / total
    out = mixed * jnp.transpose(factor, (1, 2, 0))[:, :, :, None]
    return out.astype(jnp.bfloat16).reshape(rows, heads, width)


def shards(
    queries,
    key_vectors,
    value_vectors,
    labels,
    block_lists,
    counts,
    query_scale,
    key_scale,
    value_scale,
):
    groups = lax.axis_size("x")
    halves = lax.axis_size("zh")
    frames = lax.axis_size("frame")
    quarters = lax.axis_size("quarter")
    tokens_here = queries.shape[0]
    head_count = labels.shape[0]
    width = queries.shape[1] // head_count
    per_group = head_count // groups
    lines_per_group = TEMPORAL // groups
    spaces_per_group = per_group - lines_per_group
    rows = tokens_here * groups
    blocks = rows // BLOCK
    piece = rows // frames
    chunks = frames * quarters * halves

    group_index = lax.axis_index("x")
    half_index = lax.axis_index("zh")
    frame_index = lax.axis_index("frame")
    quarter_index = lax.axis_index("quarter")
    spatial_slot = (frame_index * quarters + quarter_index) * halves + half_index
    own_piece = (frame_index % 2) * (frames // 2) + frame_index // 2
    temporal_slot = (quarter_index * halves + half_index) * frames + own_piece

    heads = jnp.arange(head_count, dtype=jnp.int32)
    earlier = heads[None, :] < heads[:, None]
    is_line = labels == 1
    line_rank = jnp.sum(jnp.where(earlier, is_line[None, :], False), axis=1, dtype=jnp.int32)
    space_rank = heads - line_rank
    unslots = jnp.where(
        is_line,
        (line_rank // lines_per_group) * per_group + line_rank % lines_per_group,
        (space_rank // spaces_per_group) * per_group + lines_per_group + space_rank % spaces_per_group,
    )
    slots = jnp.sum(jnp.where(unslots[None, :] == heads[:, None], heads[None, :], 0), axis=1)

    tile_rows = 8
    tiles = tokens_here // tile_rows

    def tiled(array):
        return jnp.transpose(array.reshape(tiles, tile_rows, head_count, width), (0, 2, 1, 3))

    columns = jnp.concatenate([tiled(queries), tiled(key_vectors), tiled(value_vectors)], axis=1)
    grid = slots.reshape(groups, per_group)
    lo, hi = slice(0, lines_per_group), slice(lines_per_group, per_group)
    order = jnp.concatenate(
        [grid[:, lo] + t * head_count for t in range(3)] + [grid[:, hi] + t * head_count for t in range(3)],
        axis=1,
    )
    picks = (
        order[:, :, None] == jnp.arange(3 * head_count, dtype=jnp.int32)[None, None, :]
    ).astype(jnp.bfloat16)
    stacked = jnp.einsum(
        "gsh,ahrd->garsd", picks, columns, preferred_element_type=jnp.bfloat16
    ).reshape(groups, tokens_here, 3 * per_group, width)
    frame_rows = lax.all_to_all(stacked, "x", split_axis=0, concat_axis=0, tiled=True)
    frame_rows = frame_rows.reshape(rows, 3 * per_group, width)
    line_part = frame_rows[:, : 3 * lines_per_group]
    space_part = frame_rows[:, 3 * lines_per_group :]
    pairs = 2
    rings = frames // pairs
    pieces = line_part.reshape(pairs, rings, piece, 3 * lines_per_group, width)
    moved = lax.all_to_all(
        jnp.transpose(pieces, (1, 0, 2, 3, 4)).reshape(frames, piece, 3 * lines_per_group, width),
        "frame",
        split_axis=0,
        concat_axis=0,
        tiled=True,
    )
    space_kv = space_part[:, spaces_per_group:]
    moved, space_kv = lax.optimization_barrier((moved, space_kv))
    line_rows = jnp.transpose(moved, (1, 0, 2, 3)).reshape(rows, 3 * lines_per_group, width)

    def linear(half, frame, quarter):
        return (half * frames + frame) * quarters + quarter

    spatial_order = [
        linear(k % halves, k // (halves * quarters), (k // halves) % quarters) for k in range(chunks)
    ]
    temporal_order = [
        linear((k // frames) % halves, (k % rings) * pairs + (k % frames) // rings, k // (frames * halves))
        for k in range(chunks)
    ]
    along = ("zh", "frame", "quarter")
    space_ext = with_halo(space_kv, along, spatial_order)
    line_ext = with_halo(line_rows[:, lines_per_group:], along, temporal_order)

    group_heads = lax.dynamic_slice_in_dim(slots, group_index * per_group, per_group)
    logit_scale = (
        jnp.take(query_scale, group_heads) * jnp.take(key_scale, group_heads) / math.sqrt(width)
    )
    value_factor = jnp.take(value_scale, group_heads)

    def run(part_rows, ext, heads, base):
        n = heads.stop - heads.start
        ids = group_heads[heads]
        allowed = window_mask(
            block_lists, counts, ids, jnp.full((n,), base * blocks, jnp.int32), blocks
        )
        return attend(
            part_rows[:, :n], ext[:, :n], ext[:, n:], allowed, logit_scale[heads], value_factor[heads]
        )

    line_out = run(line_rows, line_ext, lo, temporal_slot)
    back = jnp.transpose(line_out.reshape(piece, frames, lines_per_group, width), (1, 0, 2, 3))
    space_out = run(space_part, space_ext, hi, spatial_slot)

    returned = lax.all_to_all(back, "frame", split_axis=0, concat_axis=0, tiled=True)
    returned = jnp.transpose(
        returned.reshape(rings, pairs, piece, lines_per_group, width), (1, 0, 2, 3, 4)
    ).reshape(rows, lines_per_group, width)
    frame_outputs = jnp.concatenate([returned, space_out], axis=1)
    merged = lax.all_to_all(
        frame_outputs.reshape(groups, tokens_here, per_group, width),
        "x",
        split_axis=0,
        concat_axis=0,
        tiled=True,
    )
    places = (
        unslots[:, None] == jnp.arange(head_count, dtype=jnp.int32)[None, :]
    ).astype(jnp.bfloat16).reshape(head_count, groups, per_group)
    merged = jnp.einsum("hgs,gtsd->thd", places, merged, preferred_element_type=jnp.bfloat16)
    return merged.reshape(tokens_here, head_count * width)


def solution(mesh):
    ulysses, context = mesh.devices.shape
    halves = mesh.devices.size // (context * HEAD_SPLIT)
    fine = Mesh(
        mesh.devices.reshape(halves, HEAD_SPLIT, FRAMES, context // FRAMES),
        ("zh", "x", "frame", "quarter"),
    )
    rows = P(("frame", "quarter", "zh", "x"), None)
    placed = (rows, rows, rows, P(), P(), P(), P(), P(), P())
    return jax.shard_map(
        shards,
        mesh=fine,
        in_specs=placed,
        out_specs=rows,
        check_vma=False,
    )
```

```python
import math

import jax
import jax.numpy as jnp
from jax import lax
from jax.sharding import Mesh, PartitionSpec as P

FRAMES = 16
MARGIN = 2
BLOCK = 64
TEMPORAL = 16
HEAD_SPLIT = 4


def with_halo(cells, axes, order):
    width = MARGIN * BLOCK
    pairs = list(zip(order[:-1], order[1:]))
    lower = lax.ppermute(cells[-width:], axes, pairs)
    upper = lax.ppermute(cells[:width], axes, [(b, a) for a, b in pairs])
    return jnp.concatenate([lower, cells, upper], axis=0)


def window_mask(block_lists, counts, head_ids, base, blocks):
    span = 2 * MARGIN + 1
    list_length = block_lists.shape[2]
    head_lists = jnp.take(block_lists, head_ids, axis=0)
    head_counts = jnp.take(counts, head_ids, axis=0)
    global_ids = base[:, None] + jnp.arange(blocks, dtype=jnp.int32)[None, :]
    lists = jnp.take_along_axis(head_lists, global_ids[:, :, None], axis=1)
    used = jnp.take_along_axis(head_counts, global_ids, axis=1)
    wanted = global_ids[:, :, None] + jnp.arange(span, dtype=jnp.int32)[None, None, :] - MARGIN
    live = jnp.arange(list_length, dtype=jnp.int32)[None, None, :] < used[:, :, None]
    hit = (lists[:, :, None, :] == wanted[:, :, :, None]) & live[:, :, None, :]
    return jnp.any(hit, axis=-1)


def attend(query_rows, key_ext, value_ext, allowed, logit_scale, value_factor):
    rows, heads, width = query_rows.shape
    blocks = rows // BLOCK
    span = 2 * MARGIN + 1
    q = query_rows.reshape(blocks, BLOCK, heads, width)
    kb = key_ext.reshape(blocks + 2 * MARGIN, BLOCK, heads, width)
    vb = value_ext.reshape(blocks + 2 * MARGIN, BLOCK, heads, width)
    kw = jnp.stack([kb[o : o + blocks] for o in range(span)], axis=1)
    vw = jnp.stack([vb[o : o + blocks] for o in range(span)], axis=1)
    logits = jnp.einsum("bqhd,bokhd->hbqok", q, kw, preferred_element_type=jnp.float32)
    logits = logits * logit_scale[:, None, None, None, None]
    logits = jnp.where(allowed[:, :, None, :, None], logits, -jnp.inf)
    peak = jnp.max(logits, axis=(3, 4), keepdims=True)
    weight = jnp.exp(logits - peak)
    total = jnp.sum(weight, axis=(3, 4))
    mixed = jnp.einsum(
        "hbqok,bokhd->bqhd", weight.astype(jnp.bfloat16), vw, preferred_element_type=jnp.float32
    )
    factor = value_factor[:, None, None] / total
    out = mixed * jnp.transpose(factor, (1, 2, 0))[:, :, :, None]
    return out.astype(jnp.bfloat16).reshape(rows, heads, width)


def shards(
    queries,
    key_vectors,
    value_vectors,
    labels,
    block_lists,
    counts,
    query_scale,
    key_scale,
    value_scale,
):
    groups = lax.axis_size("x")
    halves = lax.axis_size("zh")
    frames = lax.axis_size("frame")
    quarters = lax.axis_size("quarter")
    tokens_here = queries.shape[0]
    head_count = labels.shape[0]
    width = queries.shape[1] // head_count
    per_group = head_count // groups
    lines_per_group = TEMPORAL // groups
    spaces_per_group = per_group - lines_per_group
    rows = tokens_here * groups
    blocks = rows // BLOCK
    piece = rows // frames
    chunks = frames * quarters * halves

    group_index = lax.axis_index("x")
    half_index = lax.axis_index("zh")
    frame_index = lax.axis_index("frame")
    quarter_index = lax.axis_index("quarter")
    spatial_slot = (frame_index * quarters + quarter_index) * halves + half_index
    own_piece = (frame_index % 2) * (frames // 2) + frame_index // 2
    temporal_slot = (quarter_index * halves + half_index) * frames + own_piece

    heads = jnp.arange(head_count, dtype=jnp.int32)
    earlier = heads[None, :] < heads[:, None]
    is_line = labels == 1
    line_rank = jnp.sum(jnp.where(earlier, is_line[None, :], False), axis=1, dtype=jnp.int32)
    space_rank = heads - line_rank
    unslots = jnp.where(
        is_line,
        (line_rank // lines_per_group) * per_group + line_rank % lines_per_group,
        (space_rank // spaces_per_group) * per_group + lines_per_group + space_rank % spaces_per_group,
    )
    slots = jnp.sum(jnp.where(unslots[None, :] == heads[:, None], heads[None, :], 0), axis=1)

    tile_rows = 8
    tiles = tokens_here // tile_rows

    def tiled(array):
        return jnp.transpose(array.reshape(tiles, tile_rows, head_count, width), (0, 2, 1, 3))

    columns = jnp.concatenate([tiled(queries), tiled(key_vectors), tiled(value_vectors)], axis=1)
    grid = slots.reshape(groups, per_group)
    lo, hi = slice(0, lines_per_group), slice(lines_per_group, per_group)
    order = jnp.concatenate(
        [grid[:, lo] + t * head_count for t in range(3)] + [grid[:, hi] + t * head_count for t in range(3)],
        axis=1,
    )
    picks = (
        order[:, :, None] == jnp.arange(3 * head_count, dtype=jnp.int32)[None, None, :]
    ).astype(jnp.bfloat16)
    stacked = jnp.einsum(
        "gsh,ahrd->garsd", picks, columns, preferred_element_type=jnp.bfloat16
    ).reshape(groups, tokens_here, 3 * per_group, width)
    frame_rows = lax.all_to_all(stacked, "x", split_axis=0, concat_axis=0, tiled=True)
    frame_rows = frame_rows.reshape(rows, 3 * per_group, width)
    line_part = frame_rows[:, : 3 * lines_per_group]
    space_part = frame_rows[:, 3 * lines_per_group :]
    pairs = 2
    rings = frames // pairs
    pieces = line_part.reshape(pairs, rings, piece, 3 * lines_per_group, width)
    moved = lax.all_to_all(
        jnp.transpose(pieces, (1, 0, 2, 3, 4)).reshape(frames, piece, 3 * lines_per_group, width),
        "frame",
        split_axis=0,
        concat_axis=0,
        tiled=True,
    )
    space_kv = space_part[:, spaces_per_group:]
    line_rows = jnp.transpose(moved, (1, 0, 2, 3)).reshape(rows, 3 * lines_per_group, width)

    def linear(half, frame, quarter):
        return (half * frames + frame) * quarters + quarter

    spatial_order = [
        linear(k % halves, k // (halves * quarters), (k // halves) % quarters) for k in range(chunks)
    ]
    temporal_order = [
        linear((k // frames) % halves, (k % rings) * pairs + (k % frames) // rings, k // (frames * halves))
        for k in range(chunks)
    ]
    along = ("zh", "frame", "quarter")
    space_ext = with_halo(space_kv, along, spatial_order)
    line_ext = with_halo(line_rows[:, lines_per_group:], along, temporal_order)

    group_heads = lax.dynamic_slice_in_dim(slots, group_index * per_group, per_group)
    logit_scale = (
        jnp.take(query_scale, group_heads) * jnp.take(key_scale, group_heads) / math.sqrt(width)
    )
    value_factor = jnp.take(value_scale, group_heads)

    def run(part_rows, ext, heads, base):
        n = heads.stop - heads.start
        ids = group_heads[heads]
        allowed = window_mask(
            block_lists, counts, ids, jnp.full((n,), base * blocks, jnp.int32), blocks
        )
        return attend(
            part_rows[:, :n], ext[:, :n], ext[:, n:], allowed, logit_scale[heads], value_factor[heads]
        )

    line_out = run(line_rows, line_ext, lo, temporal_slot)
    back = jnp.transpose(line_out.reshape(piece, frames, lines_per_group, width), (1, 0, 2, 3))
    space_out = run(space_part, space_ext, hi, spatial_slot)

    returned = lax.all_to_all(back, "frame", split_axis=0, concat_axis=0, tiled=True)
    returned = jnp.transpose(
        returned.reshape(rings, pairs, piece, lines_per_group, width), (1, 0, 2, 3, 4)
    ).reshape(rows, lines_per_group, width)
    frame_outputs = jnp.concatenate([returned, space_out], axis=1)
    merged = lax.all_to_all(
        frame_outputs.reshape(groups, tokens_here, per_group, width),
        "x",
        split_axis=0,
        concat_axis=0,
        tiled=True,
    )
    places = (
        unslots[:, None] == jnp.arange(head_count, dtype=jnp.int32)[None, :]
    ).astype(jnp.bfloat16).reshape(head_count, groups, per_group)
    merged = jnp.einsum("hgs,gtsd->thd", places, merged, preferred_element_type=jnp.bfloat16)
    return merged.reshape(tokens_here, head_count * width)


def solution(mesh):
    ulysses, context = mesh.devices.shape
    halves = mesh.devices.size // (context * HEAD_SPLIT)
    fine = Mesh(
        mesh.devices.reshape(halves, HEAD_SPLIT, FRAMES, context // FRAMES),
        ("zh", "x", "frame", "quarter"),
    )
    rows = P(("frame", "quarter", "zh", "x"), None)
    placed = (rows, rows, rows, P(), P(), P(), P(), P(), P())
    return jax.shard_map(
        shards,
        mesh=fine,
        in_specs=placed,
        out_specs=rows,
        check_vma=False,
    )
```

```python
import math

import jax
import jax.numpy as jnp
from jax import lax
from jax.sharding import Mesh, PartitionSpec as P

FRAMES = 16
MARGIN = 2
BLOCK = 64
TEMPORAL = 16
HEAD_SPLIT = 4


def with_halo(cells, axes, order):
    width = MARGIN * BLOCK
    pairs = list(zip(order[:-1], order[1:]))
    lower = lax.ppermute(cells[-width:], axes, pairs)
    upper = lax.ppermute(cells[:width], axes, [(b, a) for a, b in pairs])
    return jnp.concatenate([lower, cells, upper], axis=0)


def window_mask(block_lists, counts, head_ids, base, blocks):
    span = 2 * MARGIN + 1
    list_length = block_lists.shape[2]
    head_lists = jnp.take(block_lists, head_ids, axis=0)
    head_counts = jnp.take(counts, head_ids, axis=0)
    global_ids = base[:, None] + jnp.arange(blocks, dtype=jnp.int32)[None, :]
    lists = jnp.take_along_axis(head_lists, global_ids[:, :, None], axis=1)
    used = jnp.take_along_axis(head_counts, global_ids, axis=1)
    wanted = global_ids[:, :, None] + jnp.arange(span, dtype=jnp.int32)[None, None, :] - MARGIN
    live = jnp.arange(list_length, dtype=jnp.int32)[None, None, :] < used[:, :, None]
    hit = (lists[:, :, None, :] == wanted[:, :, :, None]) & live[:, :, None, :]
    return jnp.any(hit, axis=-1)


def attend(query_rows, key_ext, value_ext, allowed, logit_scale, value_factor):
    rows, heads, width = query_rows.shape
    blocks = rows // BLOCK
    span = 2 * MARGIN + 1
    q = query_rows.reshape(blocks, BLOCK, heads, width)
    kb = key_ext.reshape(blocks + 2 * MARGIN, BLOCK, heads, width)
    vb = value_ext.reshape(blocks + 2 * MARGIN, BLOCK, heads, width)
    logits = jnp.stack(
        [
            jnp.einsum("bqhd,bkhd->hbqk", q, kb[o : o + blocks], preferred_element_type=jnp.float32)
            for o in range(span)
        ],
        axis=3,
    )
    logits = logits * logit_scale[:, None, None, None, None]
    logits = jnp.where(allowed[:, :, None, :, None], logits, -jnp.inf)
    peak = jnp.max(logits, axis=(3, 4), keepdims=True)
    weight = jnp.exp(logits - peak)
    total = jnp.sum(weight, axis=(3, 4))
    weight_b = weight.astype(jnp.bfloat16)
    mixed = sum(
        jnp.einsum(
            "hbqk,bkhd->bqhd", weight_b[:, :, :, o], vb[o : o + blocks], preferred_element_type=jnp.float32
        )
        for o in range(span)
    )
    factor = value_factor[:, None, None] / total
    out = mixed * jnp.transpose(factor, (1, 2, 0))[:, :, :, None]
    return out.astype(jnp.bfloat16).reshape(rows, heads, width)


def shards(
    queries,
    key_vectors,
    value_vectors,
    labels,
    block_lists,
    counts,
    query_scale,
    key_scale,
    value_scale,
):
    groups = lax.axis_size("x")
    halves = lax.axis_size("zh")
    frames = lax.axis_size("frame")
    quarters = lax.axis_size("quarter")
    tokens_here = queries.shape[0]
    head_count = labels.shape[0]
    width = queries.shape[1] // head_count
    per_group = head_count // groups
    lines_per_group = TEMPORAL // groups
    spaces_per_group = per_group - lines_per_group
    rows = tokens_here * groups
    blocks = rows // BLOCK
    piece = rows // frames
    chunks = frames * quarters * halves

    group_index = lax.axis_index("x")
    half_index = lax.axis_index("zh")
    frame_index = lax.axis_index("frame")
    quarter_index = lax.axis_index("quarter")
    spatial_slot = (frame_index * quarters + quarter_index) * halves + half_index
    own_piece = (frame_index % 2) * (frames // 2) + frame_index // 2
    temporal_slot = (quarter_index * halves + half_index) * frames + own_piece

    heads = jnp.arange(head_count, dtype=jnp.int32)
    earlier = heads[None, :] < heads[:, None]
    is_line = labels == 1
    line_rank = jnp.sum(jnp.where(earlier, is_line[None, :], False), axis=1, dtype=jnp.int32)
    space_rank = heads - line_rank
    unslots = jnp.where(
        is_line,
        (line_rank // lines_per_group) * per_group + line_rank % lines_per_group,
        (space_rank // spaces_per_group) * per_group + lines_per_group + space_rank % spaces_per_group,
    )
    slots = jnp.sum(jnp.where(unslots[None, :] == heads[:, None], heads[None, :], 0), axis=1)

    tile_rows = 8
    tiles = tokens_here // tile_rows

    def tiled(array):
        return jnp.transpose(array.reshape(tiles, tile_rows, head_count, width), (0, 2, 1, 3))

    columns = jnp.concatenate([tiled(queries), tiled(key_vectors), tiled(value_vectors)], axis=1)
    grid = slots.reshape(groups, per_group)
    lo, hi = slice(0, lines_per_group), slice(lines_per_group, per_group)
    order = jnp.concatenate(
        [grid[:, lo] + t * head_count for t in range(3)] + [grid[:, hi] + t * head_count for t in range(3)],
        axis=1,
    )
    picks = (
        order[:, :, None] == jnp.arange(3 * head_count, dtype=jnp.int32)[None, None, :]
    ).astype(jnp.bfloat16)
    stacked = jnp.einsum(
        "gsh,ahrd->garsd", picks, columns, preferred_element_type=jnp.bfloat16
    ).reshape(groups, tokens_here, 3 * per_group, width)
    frame_rows = lax.all_to_all(stacked, "x", split_axis=0, concat_axis=0, tiled=True)
    frame_rows = frame_rows.reshape(rows, 3 * per_group, width)
    line_part = frame_rows[:, : 3 * lines_per_group]
    space_part = frame_rows[:, 3 * lines_per_group :]
    pairs = 2
    rings = frames // pairs
    pieces = line_part.reshape(pairs, rings, piece, 3 * lines_per_group, width)
    moved = lax.all_to_all(
        jnp.transpose(pieces, (1, 0, 2, 3, 4)).reshape(frames, piece, 3 * lines_per_group, width),
        "frame",
        split_axis=0,
        concat_axis=0,
        tiled=True,
    )
    space_kv = space_part[:, spaces_per_group:]
    moved, space_kv = lax.optimization_barrier((moved, space_kv))
    line_rows = jnp.transpose(moved, (1, 0, 2, 3)).reshape(rows, 3 * lines_per_group, width)

    def linear(half, frame, quarter):
        return (half * frames + frame) * quarters + quarter

    spatial_order = [
        linear(k % halves, k // (halves * quarters), (k // halves) % quarters) for k in range(chunks)
    ]
    temporal_order = [
        linear((k // frames) % halves, (k % rings) * pairs + (k % frames) // rings, k // (frames * halves))
        for k in range(chunks)
    ]
    along = ("zh", "frame", "quarter")
    space_ext = with_halo(space_kv, along, spatial_order)
    line_ext = with_halo(line_rows[:, lines_per_group:], along, temporal_order)

    group_heads = lax.dynamic_slice_in_dim(slots, group_index * per_group, per_group)
    logit_scale = (
        jnp.take(query_scale, group_heads) * jnp.take(key_scale, group_heads) / math.sqrt(width)
    )
    value_factor = jnp.take(value_scale, group_heads)

    def run(part_rows, ext, heads, base):
        n = heads.stop - heads.start
        ids = group_heads[heads]
        allowed = window_mask(
            block_lists, counts, ids, jnp.full((n,), base * blocks, jnp.int32), blocks
        )
        return attend(
            part_rows[:, :n], ext[:, :n], ext[:, n:], allowed, logit_scale[heads], value_factor[heads]
        )

    line_out = run(line_rows, line_ext, lo, temporal_slot)
    back = jnp.transpose(line_out.reshape(piece, frames, lines_per_group, width), (1, 0, 2, 3))
    space_out = run(space_part, space_ext, hi, spatial_slot)

    returned = lax.all_to_all(back, "frame", split_axis=0, concat_axis=0, tiled=True)
    returned = jnp.transpose(
        returned.reshape(rings, pairs, piece, lines_per_group, width), (1, 0, 2, 3, 4)
    ).reshape(rows, lines_per_group, width)
    frame_outputs = jnp.concatenate([returned, space_out], axis=1)
    merged = lax.all_to_all(
        frame_outputs.reshape(groups, tokens_here, per_group, width),
        "x",
        split_axis=0,
        concat_axis=0,
        tiled=True,
    )
    places = (
        unslots[:, None] == jnp.arange(head_count, dtype=jnp.int32)[None, :]
    ).astype(jnp.bfloat16).reshape(head_count, groups, per_group)
    merged = jnp.einsum("hgs,gtsd->thd", places, merged, preferred_element_type=jnp.bfloat16)
    return merged.reshape(tokens_here, head_count * width)


def solution(mesh):
    ulysses, context = mesh.devices.shape
    halves = mesh.devices.size // (context * HEAD_SPLIT)
    fine = Mesh(
        mesh.devices.reshape(halves, HEAD_SPLIT, FRAMES, context // FRAMES),
        ("zh", "x", "frame", "quarter"),
    )
    rows = P(("frame", "quarter", "zh", "x"), None)
    placed = (rows, rows, rows, P(), P(), P(), P(), P(), P())
    return jax.shard_map(
        shards,
        mesh=fine,
        in_specs=placed,
        out_specs=rows,
        check_vma=False,
    )
```
